512 devices in a mesh: seq: 64 (over x, z, core), kvh: 4 (over y_hi), rep: 2 (over y_lo).
Axes of the slice: x: 4, y: 8 (y_hi: 4, y_lo: 2; y = y_hi * 2 + y_lo), z: 8, core: 2. Of those that a mesh axis runs over, the one named last changes fastest.
Arguments:
- vision_states: bfloat16 [64, 384, 1152], P('seq', 'kvh'), may hold values from -24 to 24
- frame_tokens: int32 [64], replicated, may hold values from 128 to 384, as said below
- norm_gain: float32 [1152], replicated, may hold values from 0.1 to 1.9
- projector: bfloat16 [1152, 3584], P(None, ('kvh', 'rep')), may hold values from -0.1875 to 0.1875
- head_weights: bfloat16 [3584, 3072], P(('kvh', 'rep')), may hold values from -4 to 4
Outputs:
- attended: bfloat16 [256, 64, 2048], P(None, 'seq', ('kvh', 'rep'))
The draws below stay inside these ranges and needn't reach their ends.
Inputs may be any that keep to these rules, and one draw needn't show every extreme that they name: `frame_tokens`: the counts sum to 16384, and some frame has exactly 384 tokens.
All inputs are finite; a program needn't handle non-finite values.
Results may differ from the reference program's by a relative error of at most 0.0062.
Values may be sent and summed in bfloat16 or wider, within the bound.
No kernel may reach another device: no remote copies, remote signals or barrier semaphores. Data moves between devices by JAX's collectives and lax.ppermute only.
A program may use at most 128 MiB of HBM per device.

```python
import math
import jax
import jax.numpy as jnp
from jax import lax

VIS_WIDTH = 1152
WIDTH = 3584
KV_HEADS = 4
HEAD_DIM = 128
GROUP_HEADS = 4
FRAME_MAX = 384
FRAMES = 64
TOK_DEV = 256
TOKENS = 16384
SHARDS = 64
HEADS = 16


def draw_frame_tokens(key, part):
    lowest = FRAME_MAX // 3
    middle = 2 * FRAME_MAX // 3
    first = jax.random.randint(jax.random.fold_in(key, 11), (FRAMES // 2,), lowest, FRAME_MAX + 1, dtype=jnp.int32)
    first = first.at[0].set(FRAME_MAX)
    paired = jnp.concatenate([first, 2 * middle - first])
    order = jax.random.permutation(jax.random.fold_in(key, 12), FRAMES)
    return paired[order].astype(jnp.int32)


def draw_vision_states(key, part):
    shape = (FRAMES, FRAME_MAX, VIS_WIDTH)
    channel_scale = jnp.exp(jax.random.uniform(jax.random.fold_in(key, 21), (VIS_WIDTH,), jnp.float32, -0.7, 0.7))
    channel_mean = 0.5 * jax.random.normal(jax.random.fold_in(key, 22), (VIS_WIDTH,), jnp.float32)
    base = jax.random.normal(jax.random.fold_in(key, 23), shape, jnp.float32)
    values = base * channel_scale + channel_mean
    return jnp.clip(values, -24.0, 24.0).astype(jnp.bfloat16)


def draw_head_weights(key, part):
    shape = (WIDTH, KV_HEADS, GROUP_HEADS + 2, HEAD_DIM)
    base = jnp.clip(jax.random.normal(jax.random.fold_in(key, 31), shape, jnp.float32), -6.0, 6.0) * WIDTH ** (-0.5)
    column_kind = jnp.arange(GROUP_HEADS + 2)
    column_scale = jnp.where(column_kind < GROUP_HEADS + 1, 2.5, 1.0)
    weights = base * column_scale[None, None, :, None]
    weights = jnp.clip(weights, -4.0, 4.0)
    return weights.reshape(WIDTH, KV_HEADS * (GROUP_HEADS + 2) * HEAD_DIM).astype(jnp.bfloat16)


def block_levels(stream_key, shape, cuts, least, top_value):
    level, own = 1.0, jax.random.fold_in(stream_key, 6)
    for dim, shards_of in cuts:
        draws = jnp.exp(jax.random.uniform(jax.random.fold_in(own, dim), (shards_of,), jnp.float32, least / len(cuts), top_value / len(cuts)))
        level = level * jnp.repeat(draws, shape[dim] // shards_of).reshape([-1 if axis == dim else 1 for axis in range(len(shape))])
    return level


def normal_values(rng, extent, deviation, limit, shards=(), held_as=jnp.bfloat16):
    result = jax.random.normal(rng, extent, jnp.float32) * deviation
    if len(shards) > 0:
        result = block_levels(rng, extent, shards, -0.22, 0.18) * result
    return jnp.clip(result, min=-limit, max=limit).astype(held_as)


def setup_inputs(seed: int = 0) -> dict:
    streams_of = jax.random.split(jax.random.key(seed), 6)
    return {
        "vision_states": draw_vision_states(jax.random.fold_in(streams_of[5], 71), 0),
        "frame_tokens": draw_frame_tokens(jax.random.fold_in(streams_of[5], 71), 0),
        "norm_gain": jnp.clip(1.0 + 0.18 * jax.random.normal(streams_of[2], (VIS_WIDTH,), jnp.float32), 0.1, 1.9),
        "projector": normal_values(streams_of[3], (VIS_WIDTH, WIDTH), VIS_WIDTH ** -0.5, 0.1875, ((1, 8),)),
        "head_weights": draw_head_weights(jax.random.fold_in(streams_of[5], 71), 0),
    }


norm_eps = 1e-06

def layer_norm(states, norm_gain):
    values = states.astype(jnp.float32)
    center = values - lax.optimization_barrier(jnp.mean(values, axis=-1, keepdims=True))
    spread = lax.optimization_barrier(jnp.mean(center * center, axis=-1, keepdims=True))
    return (center * lax.rsqrt(spread + norm_eps) * norm_gain).astype(jnp.bfloat16)

def reference(vision_states, frame_tokens, norm_gain, projector, head_weights):
    normed = layer_norm(vision_states, norm_gain)
    hidden = jnp.dot(normed.reshape(FRAMES * FRAME_MAX, VIS_WIDTH), projector, preferred_element_type=jnp.float32)
    visual_frames = jax.nn.gelu(hidden, approximate=False).astype(jnp.bfloat16)
    counts = frame_tokens.astype(jnp.int32)
    ends = jnp.cumsum(counts).astype(jnp.int32)
    position = jnp.arange(TOKENS, dtype=jnp.int32)
    before = ends[None, :] <= position[:, None]
    frame = lax.optimization_barrier(jnp.sum(before.astype(jnp.int32), axis=1)).astype(jnp.int32)
    offset = lax.optimization_barrier(jnp.sum(jnp.where(before, counts[None, :], 0), axis=1)).astype(jnp.int32)
    row_index = (frame * FRAME_MAX + position - offset).astype(jnp.int32)
    visual = visual_frames[row_index]
    heads_all = jnp.dot(visual, head_weights, preferred_element_type=jnp.float32).astype(jnp.bfloat16)
    heads_all = heads_all.reshape(TOKENS, KV_HEADS, GROUP_HEADS + 2, HEAD_DIM)
    queries = heads_all[:, :, :GROUP_HEADS]
    keys = heads_all[:, :, GROUP_HEADS].astype(jnp.float32)
    values = heads_all[:, :, GROUP_HEADS + 1].astype(jnp.float32)
    scale = HEAD_DIM ** (-0.5)
    block = math.gcd(TOKENS, 512)

    def one_block(index):
        first = index * block
        rows_here = lax.dynamic_slice_in_dim(queries, first, block, 0).astype(jnp.float32)
        scores = jnp.einsum('bgnh,egh->bgne', rows_here, keys) * scale
        query_pos = first + jnp.arange(block, dtype=jnp.int32)
        allowed = (position[None, :] <= query_pos[:, None])[:, None, None, :]
        top = lax.optimization_barrier(jnp.max(jnp.where(allowed, scores, -jnp.inf), axis=-1, keepdims=True))
        weights = jnp.where(allowed, jnp.exp(scores - top), 0.0)
        total = lax.optimization_barrier(jnp.sum(weights, axis=-1))
        rounded = lax.optimization_barrier(weights.astype(jnp.bfloat16)).astype(jnp.float32)
        context = jnp.einsum('bgne,egh->bgnh', rounded, values)
        return (context / total[..., None]).astype(jnp.bfloat16)
    attended = lax.map(one_block, jnp.arange(TOKENS // block, dtype=jnp.int32))
    return attended.reshape(TOK_DEV, SHARDS, HEADS * HEAD_DIM)
```

```python
import jax
import jax.numpy as jnp
from jax import lax
from jax.sharding import PartitionSpec as P

KV_HEADS = 4
HEAD_DIM = 128
GROUP_HEADS = 4


norm_eps = 1e-06
masked_score = -1e30


def layer_norm(states, norm_gain):
    values = states.astype(jnp.float32)
    center = values - jnp.mean(values, axis=-1, keepdims=True)
    spread = jnp.mean(center * center, axis=-1, keepdims=True)
    return (center * lax.rsqrt(spread + norm_eps) * norm_gain).astype(jnp.bfloat16)


def attention_step(queries, query_pos, key_rows, key_base, seq_count):
    scale = queries.shape[-1] ** (-0.5)

    def add_keys(carry, piece, start):
        context, top, total = carry
        key_piece, value_piece = piece
        number = key_piece.shape[0]
        index = jnp.arange(number, dtype=jnp.int32)
        key_pos = (key_base + index % key_rows) * seq_count + index // key_rows
        allowed = (key_pos[None, :] <= query_pos[:, None])[:, None, :]
        scores = (
            jnp.einsum("qhd,kd->qhk", queries, key_piece, preferred_element_type=jnp.float32)
            * scale
        )
        scores = jnp.where(allowed, scores, masked_score)
        new_top = jnp.maximum(top, jnp.max(scores, axis=-1))
        weights = jnp.where(allowed, jnp.exp(scores - new_top[..., None]), 0.0)
        total = jnp.sum(weights, axis=-1)
        update = jnp.einsum(
            "qhk,kd->qhd",
            weights.astype(jnp.bfloat16),
            value_piece,
            preferred_element_type=jnp.float32,
        )
        return (update, new_top, total)

    return add_keys


def empty_partials(tok_rows, head_count):
    return (
        jnp.zeros((tok_rows, head_count, HEAD_DIM), jnp.float32),
        jnp.full((tok_rows, head_count), masked_score, jnp.float32),
        jnp.zeros((tok_rows, head_count), jnp.float32),
    )


def local(vision_states, frame_tokens, norm_gain, projector, head_weights):
    seq_count = lax.axis_size("seq")
    seq_index = lax.axis_index("seq")
    rep_count = lax.axis_size("rep")
    frames_dev = vision_states.shape[0]
    frame_max = vision_states.shape[1] * lax.axis_size("kvh")
    d_cols = projector.shape[1]
    cap_frame = frame_max // seq_count
    tok_rows = 2 * frames_dev * frame_max // 3
    heads_local = GROUP_HEADS // rep_count
    normed = layer_norm(vision_states, norm_gain)
    frame_rows = lax.all_gather(normed[0], "kvh", axis=0, tiled=False).reshape(1, frame_max, -1)
    hidden = jnp.einsum(
        "frv,vc->frc",
        frame_rows,
        projector,
        preferred_element_type=jnp.float32,
    )
    visual_frames = jax.nn.gelu(hidden, approximate=False).astype(jnp.bfloat16)
    ends = jnp.cumsum(frame_tokens)
    starts_all = ends - frame_tokens
    my_starts = lax.dynamic_slice_in_dim(starts_all, seq_index * frames_dev, frames_dev, 0)
    dest = jnp.arange(seq_count, dtype=jnp.int32)[:, None, None]
    slots = jnp.arange(cap_frame, dtype=jnp.int32)[None, None, :]
    frame_local = jnp.arange(frames_dev, dtype=jnp.int32)[None, :, None]
    row_of = jnp.mod(dest - my_starts[None, :, None], seq_count) + slots * seq_count
    send_index = (frame_local * frame_max + row_of).reshape(-1)
    outgoing = visual_frames.reshape(frames_dev * frame_max, d_cols)[send_index]
    received = lax.all_to_all(outgoing, "seq", split_axis=0, concat_axis=0, tiled=True)
    query_pos = jnp.arange(tok_rows, dtype=jnp.int32) * seq_count + seq_index
    before = ends[None, :] <= query_pos[:, None]
    frame = jnp.sum(before.astype(jnp.int32), axis=1)
    offset = jnp.sum(jnp.where(before, frame_tokens[None, :], 0), axis=1)
    slot_index = frame * cap_frame + (query_pos - offset) // seq_count
    visual = received[slot_index]
    wide = head_weights.reshape(d_cols, KV_HEADS, GROUP_HEADS + 2, HEAD_DIM)
    query_w = wide[:, :, :GROUP_HEADS].reshape(d_cols, KV_HEADS, rep_count, heads_local * HEAD_DIM)
    pair_w = wide[:, :, GROUP_HEADS:].reshape(d_cols, KV_HEADS, 1, 2 * HEAD_DIM)
    pair_w = jnp.broadcast_to(pair_w, (d_cols, KV_HEADS, rep_count, 2 * HEAD_DIM))
    piece_w = jnp.concatenate([query_w, pair_w], axis=3).reshape(
        d_cols, KV_HEADS * rep_count, (heads_local + 2) * HEAD_DIM
    )
    summed = lax.psum_scatter(
        jnp.einsum("tc,cpw->ptw", visual, piece_w, preferred_element_type=jnp.float32),
        ("kvh", "rep"),
        scatter_dimension=0,
        tiled=True,
    )[0]
    head_rows = summed.astype(jnp.bfloat16)
    queries = head_rows[:, : heads_local * HEAD_DIM].reshape(tok_rows, heads_local, HEAD_DIM)
    pair_own = head_rows[:, heads_local * HEAD_DIM :]
    pair_all = lax.all_gather(pair_own, "seq", axis=0, tiled=False)
    keys = pair_all[..., :HEAD_DIM]
    values = pair_all[..., HEAD_DIM:]
    scale = HEAD_DIM ** (-0.5)
    key_pos = (
        jnp.arange(tok_rows, dtype=jnp.int32)[None, :] * seq_count
        + jnp.arange(seq_count, dtype=jnp.int32)[:, None]
    )
    allowed = (key_pos[None, :, :] <= query_pos[:, None, None])[:, None, :, :]
    scores = (
        jnp.einsum("qhd,skd->qhsk", queries, keys, preferred_element_type=jnp.float32)
        * scale
    )
    scores = jnp.where(allowed, scores, masked_score)
    top = jnp.max(scores, axis=(2, 3))
    weights = jnp.where(allowed, jnp.exp(scores - top[..., None, None]), 0.0)
    total = jnp.sum(weights, axis=(2, 3))
    context = jnp.einsum(
        "qhsk,skd->qhd",
        weights.astype(jnp.bfloat16),
        values,
        preferred_element_type=jnp.float32,
    )
    result = (context / total[..., None]).astype(jnp.bfloat16)
    return result.reshape(tok_rows, 1, heads_local * HEAD_DIM)


def solution(mesh):
    placed = (P("seq", "kvh", None), P(), P(), P(None, ("kvh", "rep")), P(("kvh", "rep"), None))
    return jax.shard_map(
        local, mesh=mesh, in_specs=placed, out_specs=P(None, "seq", ("kvh", "rep")), check_vma=False
    )
```

```python
import functools

import jax
import jax.numpy as jnp
from jax import lax
from jax.experimental import pallas as pl
from jax.experimental.pallas import tpu as pltpu
from jax.sharding import PartitionSpec as P

KV_HEADS = 4
HEAD_DIM = 128
GROUP_HEADS = 4


norm_eps = 1e-06
masked_score = -1e30


def layer_norm(states, norm_gain):
    values = states.astype(jnp.float32)
    center = values - jnp.mean(values, axis=-1, keepdims=True)
    spread = jnp.mean(center * center, axis=-1, keepdims=True)
    return (center * lax.rsqrt(spread + norm_eps) * norm_gain).astype(jnp.bfloat16)


def attention_kernel(seq_ref, q_ref, kv_ref, o_ref, *, shards, tok_rows, block):
    seq_index = seq_ref[0]
    scale = HEAD_DIM ** (-0.5)
    rows = q_ref.shape[0] // (tok_rows // block)
    for qb in range(tok_rows // block):
        width = min(tok_rows, (qb + 1) * block)
        width = -(-width // 128) * 128
        q = q_ref[qb * rows : (qb + 1) * rows, :]
        row_j = qb * block + lax.broadcasted_iota(jnp.int32, (rows, 1), 0) % block
        query_pos = row_j * shards + seq_index
        lane_j = lax.broadcasted_iota(jnp.int32, (1, width), 1) * shards

        def body(src, carry):
            top, total, context = carry
            col = pl.multiple_of(src * tok_rows, tok_rows)
            key_t = kv_ref[:HEAD_DIM, pl.ds(col, width)]
            value_t = kv_ref[HEAD_DIM:, pl.ds(col, width)]
            scores = jnp.dot(q, key_t, preferred_element_type=jnp.float32) * scale
            allowed = (lane_j + src) <= query_pos
            scores = jnp.where(allowed, scores, masked_score)
            new_top = jnp.maximum(top, jnp.max(scores, axis=1, keepdims=True))
            shrink = jnp.exp(top - new_top)
            weights = jnp.exp(scores - new_top)
            total = shrink * total + jnp.sum(weights, axis=1, keepdims=True)
            update = lax.dot_general(
                weights.astype(jnp.bfloat16),
                value_t,
                (((1,), (1,)), ((), ())),
                preferred_element_type=jnp.float32,
            )
            return new_top, total, shrink * context + update

        start = (
            jnp.full((rows, 1), masked_score, jnp.float32),
            jnp.zeros((rows, 1), jnp.float32),
            jnp.zeros((rows, HEAD_DIM), jnp.float32),
        )
        top, total, context = lax.fori_loop(0, shards, body, start)
        o_ref[qb * rows : (qb + 1) * rows, :] = (context / total).astype(o_ref.dtype)


def causal_attention(seq_index, queries, pair_all, block=128):
    tok_rows, heads_local, _ = queries.shape
    shards = pair_all.shape[0]
    blocks = tok_rows // block
    q_rows = (
        queries.reshape(blocks, block, heads_local, HEAD_DIM)
        .transpose(0, 2, 1, 3)
        .reshape(tok_rows * heads_local, HEAD_DIM)
    )
    kv_t = pair_all.reshape(shards * tok_rows, 2 * HEAD_DIM).T
    out = pl.pallas_call(
        functools.partial(attention_kernel, shards=shards, tok_rows=tok_rows, block=block),
        out_shape=jax.ShapeDtypeStruct((tok_rows * heads_local, HEAD_DIM), jnp.bfloat16),
        in_specs=[
            pl.BlockSpec(memory_space=pltpu.SMEM),
            pl.BlockSpec(memory_space=pltpu.VMEM),
            pl.BlockSpec(memory_space=pltpu.VMEM),
        ],
        out_specs=pl.BlockSpec(memory_space=pltpu.VMEM),
        compiler_params=pltpu.CompilerParams(vmem_limit_bytes=48 * 1024 * 1024),
        cost_estimate=pl.CostEstimate(
            flops=4 * tok_rows * heads_local * shards * tok_rows * HEAD_DIM * 3 // 4,
            transcendentals=tok_rows * heads_local * shards * tok_rows * 3 // 4,
            bytes_accessed=kv_t.size * 2 + 2 * q_rows.size * 2,
        ),
    )(jnp.reshape(seq_index, (1,)).astype(jnp.int32), q_rows, kv_t)
    return (
        out.reshape(blocks, heads_local, block, HEAD_DIM)
        .transpose(0, 2, 1, 3)
        .reshape(tok_rows, 1, heads_local * HEAD_DIM)
    )


def local(vision_states, frame_tokens, norm_gain, projector, head_weights):
    seq_count = lax.axis_size("seq")
    seq_index = lax.axis_index("seq")
    rep_count = lax.axis_size("rep")
    frames_dev = vision_states.shape[0]
    frame_max = vision_states.shape[1] * lax.axis_size("kvh")
    d_cols = projector.shape[1]
    cap_frame = frame_max // seq_count
    tok_rows = 2 * frames_dev * frame_max // 3
    heads_local = GROUP_HEADS // rep_count
    normed = layer_norm(vision_states, norm_gain)
    frame_rows = lax.all_gather(normed[0], "kvh", axis=0, tiled=False).reshape(1, frame_max, -1)
    hidden = jnp.einsum(
        "frv,vc->frc",
        frame_rows,
        projector,
        preferred_element_type=jnp.float32,
    )
    visual_frames = jax.nn.gelu(hidden, approximate=False).astype(jnp.bfloat16)
    ends = jnp.cumsum(frame_tokens)
    starts_all = ends - frame_tokens
    my_starts = lax.dynamic_slice_in_dim(starts_all, seq_index * frames_dev, frames_dev, 0)
    dest = jnp.arange(seq_count, dtype=jnp.int32)[:, None, None]
    slots = jnp.arange(cap_frame, dtype=jnp.int32)[None, None, :]
    frame_local = jnp.arange(frames_dev, dtype=jnp.int32)[None, :, None]
    row_of = jnp.mod(dest - my_starts[None, :, None], seq_count) + slots * seq_count
    send_index = (frame_local * frame_max + row_of).reshape(-1)
    outgoing = visual_frames.reshape(frames_dev * frame_max, d_cols)[send_index]
    received = lax.all_to_all(outgoing, "seq", split_axis=0, concat_axis=0, tiled=True)
    query_pos = jnp.arange(tok_rows, dtype=jnp.int32) * seq_count + seq_index
    before = ends[None, :] <= query_pos[:, None]
    frame = jnp.sum(before.astype(jnp.int32), axis=1)
    offset = jnp.sum(jnp.where(before, frame_tokens[None, :], 0), axis=1)
    slot_index = frame * cap_frame + (query_pos - offset) // seq_count
    visual = received[slot_index]
    wide = head_weights.reshape(d_cols, KV_HEADS, GROUP_HEADS + 2, HEAD_DIM)
    query_w = wide[:, :, :GROUP_HEADS].reshape(d_cols, KV_HEADS, rep_count, heads_local * HEAD_DIM)
    pair_w = wide[:, :, GROUP_HEADS:].reshape(d_cols, KV_HEADS, 1, 2 * HEAD_DIM)
    pair_w = jnp.broadcast_to(pair_w, (d_cols, KV_HEADS, rep_count, 2 * HEAD_DIM))
    piece_w = jnp.concatenate([query_w, pair_w], axis=3).reshape(
        d_cols, KV_HEADS * rep_count, (heads_local + 2) * HEAD_DIM
    )
    summed = lax.psum_scatter(
        jnp.einsum("tc,cpw->ptw", visual, piece_w, preferred_element_type=jnp.float32),
        ("kvh", "rep"),
        scatter_dimension=0,
        tiled=True,
    )[0]
    head_rows = summed.astype(jnp.bfloat16)
    queries = head_rows[:, : heads_local * HEAD_DIM].reshape(tok_rows, heads_local, HEAD_DIM)
    pair_own = head_rows[:, heads_local * HEAD_DIM :]
    pair_all = lax.all_gather(pair_own, "seq", axis=0, tiled=False)
    return causal_attention(seq_index, queries, pair_all)


def solution(mesh):
    placed = (P("seq", "kvh", None), P(), P(), P(None, ("kvh", "rep")), P(("kvh", "rep"), None))
    return jax.shard_map(
        local, mesh=mesh, in_specs=placed, out_specs=P(None, "seq", ("kvh", "rep")), check_vma=False
    )
```

```python
import functools

import jax
import jax.numpy as jnp
from jax import lax
from jax.experimental import pallas as pl
from jax.experimental.pallas import tpu as pltpu
from jax.sharding import PartitionSpec as P

KV_HEADS = 4
HEAD_DIM = 128
GROUP_HEADS = 4


norm_eps = 1e-06
masked_score = -1e30
UNROLL = 8


def layer_norm(states, norm_gain):
    values = states.astype(jnp.float32)
    center = values - jnp.mean(values, axis=-1, keepdims=True)
    spread = jnp.mean(center * center, axis=-1, keepdims=True)
    return (center * lax.rsqrt(spread + norm_eps) * norm_gain).astype(jnp.bfloat16)


def attention_kernel(seq_ref, q_ref, kv_ref, o_ref, *, shards, tok_rows, block):
    seq_index = seq_ref[0]
    scale = HEAD_DIM ** (-0.5)
    rows = q_ref.shape[0] // (tok_rows // block)
    for qb in range(tok_rows // block):
        width = (((qb + 1) * block - 1) // 128 + 1) * 128
        q = q_ref[qb * rows : (qb + 1) * rows, :]
        row_j = qb * block + lax.broadcasted_iota(jnp.int32, (rows, 1), 0) % block
        query_pos = row_j * shards + seq_index
        lane_pos = lax.broadcasted_iota(jnp.int32, (1, width), 1) * shards

        def body(src, carry):
            top, total, context = carry
            col = pl.multiple_of(src * tok_rows, tok_rows)
            key_t = kv_ref[:HEAD_DIM, pl.ds(col, width)]
            value_t = kv_ref[HEAD_DIM:, pl.ds(col, width)]
            scores = jnp.dot(q, key_t, preferred_element_type=jnp.float32) * scale
            allowed = lane_pos <= query_pos - src
            scores = jnp.where(allowed, scores, masked_score)
            new_top = jnp.maximum(top, jnp.max(scores, axis=1, keepdims=True))
            shrink = jnp.exp(top - new_top)
            weights = jnp.exp(scores - new_top)
            total = shrink * total + jnp.sum(weights, axis=1, keepdims=True)
            update = lax.dot_general(
                weights.astype(jnp.bfloat16),
                value_t,
                (((1,), (1,)), ((), ())),
                preferred_element_type=jnp.float32,
            )
            return new_top, total, shrink * context + update

        start = (
            jnp.full((rows, 1), masked_score, jnp.float32),
            jnp.zeros((rows, 1), jnp.float32),
            jnp.zeros((rows, HEAD_DIM), jnp.float32),
        )
        top, total, context = lax.fori_loop(0, shards, body, start, unroll=UNROLL)
        o_ref[qb * rows : (qb + 1) * rows, :] = (context / total).astype(o_ref.dtype)


def causal_attention(seq_index, queries, pair_all, block=128):
    tok_rows, heads_local, _ = queries.shape
    shards = pair_all.shape[0]
    blocks = tok_rows // block
    q_rows = (
        queries.reshape(blocks, block, heads_local, HEAD_DIM)
        .transpose(0, 2, 1, 3)
        .reshape(tok_rows * heads_local, HEAD_DIM)
    )
    kv_t = pair_all.reshape(shards * tok_rows, 2 * HEAD_DIM).T
    out = pl.pallas_call(
        functools.partial(attention_kernel, shards=shards, tok_rows=tok_rows, block=block),
        out_shape=jax.ShapeDtypeStruct((tok_rows * heads_local, HEAD_DIM), jnp.bfloat16),
        in_specs=[
            pl.BlockSpec(memory_space=pltpu.SMEM),
            pl.BlockSpec(memory_space=pltpu.VMEM),
            pl.BlockSpec(memory_space=pltpu.VMEM),
        ],
        out_specs=pl.BlockSpec(memory_space=pltpu.VMEM),
        compiler_params=pltpu.CompilerParams(vmem_limit_bytes=48 * 1024 * 1024),
        cost_estimate=pl.CostEstimate(
            flops=4 * tok_rows * heads_local * shards * tok_rows * HEAD_DIM * 3 // 4,
            transcendentals=tok_rows * heads_local * shards * tok_rows * 3 // 4,
            bytes_accessed=kv_t.size * 2 + 2 * q_rows.size * 2,
        ),
    )(jnp.reshape(seq_index, (1,)).astype(jnp.int32), q_rows, kv_t)
    return (
        out.reshape(blocks, heads_local, block, HEAD_DIM)
        .transpose(0, 2, 1, 3)
        .reshape(tok_rows, 1, heads_local * HEAD_DIM)
    )


def local(vision_states, frame_tokens, norm_gain, projector, head_weights):
    seq_count = lax.axis_size("seq")
    seq_index = lax.axis_index("seq")
    rep_count = lax.axis_size("rep")
    frames_dev = vision_states.shape[0]
    frame_max = vision_states.shape[1] * lax.axis_size("kvh")
    d_cols = projector.shape[1]
    cap_frame = frame_max // seq_count
    tok_rows = 2 * frames_dev * frame_max // 3
    heads_local = GROUP_HEADS // rep_count
    normed = layer_norm(vision_states, norm_gain)
    frame_rows = lax.all_gather(normed[0], "kvh", axis=0, tiled=False).reshape(1, frame_max, -1)
    hidden = jnp.einsum(
        "frv,vc->frc",
        frame_rows,
        projector,
        preferred_element_type=jnp.float32,
    )
    visual_frames = jax.nn.gelu(hidden, approximate=False).astype(jnp.bfloat16)
    ends = jnp.cumsum(frame_tokens)
    starts_all = ends - frame_tokens
    my_starts = lax.dynamic_slice_in_dim(starts_all, seq_index * frames_dev, frames_dev, 0)
    dest = jnp.arange(seq_count, dtype=jnp.int32)[:, None, None]
    slots = jnp.arange(cap_frame, dtype=jnp.int32)[None, None, :]
    frame_local = jnp.arange(frames_dev, dtype=jnp.int32)[None, :, None]
    row_of = jnp.mod(dest - my_starts[None, :, None], seq_count) + slots * seq_count
    send_index = (frame_local * frame_max + row_of).reshape(-1)
    outgoing = visual_frames.reshape(frames_dev * frame_max, d_cols)[send_index]
    received = lax.all_to_all(outgoing, "seq", split_axis=0, concat_axis=0, tiled=True)
    query_pos = jnp.arange(tok_rows, dtype=jnp.int32) * seq_count + seq_index
    before = ends[None, :] <= query_pos[:, None]
    frame = jnp.sum(before.astype(jnp.int32), axis=1)
    offset = jnp.sum(jnp.where(before, frame_tokens[None, :], 0), axis=1)
    slot_index = frame * cap_frame + (query_pos - offset) // seq_count
    visual = received[slot_index]
    wide = head_weights.reshape(d_cols, KV_HEADS, GROUP_HEADS + 2, HEAD_DIM)
    query_w = wide[:, :, :GROUP_HEADS].reshape(d_cols, KV_HEADS, rep_count, heads_local * HEAD_DIM)
    pair_w = wide[:, :, GROUP_HEADS:].reshape(d_cols, KV_HEADS, 1, 2 * HEAD_DIM)
    pair_w = jnp.broadcast_to(pair_w, (d_cols, KV_HEADS, rep_count, 2 * HEAD_DIM))
    piece_w = jnp.concatenate([query_w, pair_w], axis=3).reshape(
        d_cols, KV_HEADS * rep_count, (heads_local + 2) * HEAD_DIM
    )
    summed = lax.psum_scatter(
        jnp.einsum("tc,cpw->ptw", visual, piece_w, preferred_element_type=jnp.float32),
        ("kvh", "rep"),
        scatter_dimension=0,
        tiled=True,
    )[0]
    head_rows = summed.astype(jnp.bfloat16)
    queries = head_rows[:, : heads_local * HEAD_DIM].reshape(tok_rows, heads_local, HEAD_DIM)
    pair_own = head_rows[:, heads_local * HEAD_DIM :]
    pair_all = lax.all_gather(pair_own, "seq", axis=0, tiled=False)
    return causal_attention(seq_index, queries, pair_all)


def solution(mesh):
    placed = (P("seq", "kvh", None), P(), P(), P(None, ("kvh", "rep")), P(("kvh", "rep"), None))
    return jax.shard_map(
        local, mesh=mesh, in_specs=placed, out_specs=P(None, "seq", ("kvh", "rep")), check_vma=False
    )
```

```python
import functools

import jax
import jax.numpy as jnp
from jax import lax
from jax.experimental import pallas as pl
from jax.experimental.pallas import tpu as pltpu
from jax.sharding import PartitionSpec as P

KV_HEADS = 4
HEAD_DIM = 128
GROUP_HEADS = 4


norm_eps = 1e-06
masked_score = -1e30
UNROLL = 8


def layer_norm(states, norm_gain):
    values = states.astype(jnp.float32)
    center = values - jnp.mean(values, axis=-1, keepdims=True)
    spread = jnp.mean(center * center, axis=-1, keepdims=True)
    return (center * lax.rsqrt(spread + norm_eps) * norm_gain).astype(jnp.bfloat16)


def attention_kernel(seq_ref, q_ref, kv_ref, o_ref, *, shards, tok_rows, block):
    seq_index = seq_ref[0]
    scale = HEAD_DIM ** (-0.5)
    rows = q_ref.shape[0] // (tok_rows // block)
    for qb in range(tok_rows // block):
        width = (((qb + 1) * block - 1) // 128 + 1) * 128
        q = q_ref[qb * rows : (qb + 1) * rows, :]
        row_j = qb * block + lax.broadcasted_iota(jnp.int32, (rows, 1), 0) % block
        query_pos = row_j * shards + seq_index
        lane_pos = lax.broadcasted_iota(jnp.int32, (1, width), 1) * shards

        def body(src, carry):
            top, total, context = carry
            col = pl.multiple_of(src * tok_rows, tok_rows)
            key_t = kv_ref[:HEAD_DIM, pl.ds(col, width)]
            value_t = kv_ref[HEAD_DIM:, pl.ds(col, width)]
            scores = jnp.dot(q, key_t, preferred_element_type=jnp.float32) * scale
            allowed = lane_pos <= query_pos - src
            scores = jnp.where(allowed, scores, masked_score)
            new_top = jnp.maximum(top, jnp.max(scores, axis=1, keepdims=True))
            shrink = jnp.exp(top - new_top)
            weights = jnp.exp(scores - new_top)
            total = shrink * total + jnp.sum(weights, axis=1, keepdims=True)
            update = lax.dot_general(
                weights.astype(jnp.bfloat16),
                value_t,
                (((1,), (1,)), ((), ())),
                preferred_element_type=jnp.float32,
            )
            return new_top, total, shrink * context + update

        start = (
            jnp.full((rows, 1), masked_score, jnp.float32),
            jnp.zeros((rows, 1), jnp.float32),
            jnp.zeros((rows, HEAD_DIM), jnp.float32),
        )
        top, total, context = lax.fori_loop(0, shards, body, start, unroll=UNROLL)
        o_ref[qb * rows : (qb + 1) * rows, :] = (context / total).astype(o_ref.dtype)


def causal_attention(seq_index, queries, pair_all, block=128):
    tok_rows, heads_local, _ = queries.shape
    shards = pair_all.shape[0]
    blocks = tok_rows // block
    q_rows = (
        queries.reshape(blocks, block, heads_local, HEAD_DIM)
        .transpose(0, 2, 1, 3)
        .reshape(tok_rows * heads_local, HEAD_DIM)
    )
    kv_t = pair_all.reshape(shards * tok_rows, 2 * HEAD_DIM).T
    out = pl.pallas_call(
        functools.partial(attention_kernel, shards=shards, tok_rows=tok_rows, block=block),
        out_shape=jax.ShapeDtypeStruct((tok_rows * heads_local, HEAD_DIM), jnp.bfloat16),
        in_specs=[
            pl.BlockSpec(memory_space=pltpu.SMEM),
            pl.BlockSpec(memory_space=pltpu.VMEM),
            pl.BlockSpec(memory_space=pltpu.VMEM),
        ],
        out_specs=pl.BlockSpec(memory_space=pltpu.VMEM),
        compiler_params=pltpu.CompilerParams(vmem_limit_bytes=48 * 1024 * 1024),
        cost_estimate=pl.CostEstimate(
            flops=4 * tok_rows * heads_local * shards * tok_rows * HEAD_DIM * 3 // 4,
            transcendentals=tok_rows * heads_local * shards * tok_rows * 3 // 4,
            bytes_accessed=kv_t.size * 2 + 2 * q_rows.size * 2,
        ),
    )(jnp.reshape(seq_index, (1,)).astype(jnp.int32), q_rows, kv_t)
    return (
        out.reshape(blocks, heads_local, block, HEAD_DIM)
        .transpose(0, 2, 1, 3)
        .reshape(tok_rows, 1, heads_local * HEAD_DIM)
    )


def ring_reduce_scatter(parts):
    count = parts.shape[0]
    axes = ("kvh", "rep")
    index = lax.axis_index("kvh") * lax.axis_size("rep") + lax.axis_index("rep")
    half = parts.shape[-1] // 2
    sums = []
    for step_dir, piece in ((1, parts[..., :half]), (-1, parts[..., half:])):
        perm = [(i, (i + step_dir) % count) for i in range(count)]
        buf = lax.dynamic_index_in_dim(piece, (index - step_dir) % count, 0, keepdims=False)
        for t in range(1, count):
            buf = lax.ppermute(buf, axes, perm)
            own = lax.dynamic_index_in_dim(piece, (index - step_dir * (t + 1)) % count, 0, keepdims=False)
            buf = buf + own
        sums.append(buf)
    return jnp.concatenate(sums, axis=-1)


def local(vision_states, frame_tokens, norm_gain, projector, head_weights):
    seq_count = lax.axis_size("seq")
    seq_index = lax.axis_index("seq")
    rep_count = lax.axis_size("rep")
    frames_dev = vision_states.shape[0]
    frame_max = vision_states.shape[1] * lax.axis_size("kvh")
    d_cols = projector.shape[1]
    cap_frame = frame_max // seq_count
    tok_rows = 2 * frames_dev * frame_max // 3
    heads_local = GROUP_HEADS // rep_count
    normed = layer_norm(vision_states, norm_gain)
    frame_rows = lax.all_gather(normed[0], "kvh", axis=0, tiled=False).reshape(1, frame_max, -1)
    hidden = jnp.einsum(
        "frv,vc->frc",
        frame_rows,
        projector,
        preferred_element_type=jnp.float32,
    )
    visual_frames = jax.nn.gelu(hidden, approximate=False).astype(jnp.bfloat16)
    ends = jnp.cumsum(frame_tokens)
    starts_all = ends - frame_tokens
    my_starts = lax.dynamic_slice_in_dim(starts_all, seq_index * frames_dev, frames_dev, 0)
    dest = jnp.arange(seq_count, dtype=jnp.int32)[:, None, None]
    slots = jnp.arange(cap_frame, dtype=jnp.int32)[None, None, :]
    frame_local = jnp.arange(frames_dev, dtype=jnp.int32)[None, :, None]
    row_of = jnp.mod(dest - my_starts[None, :, None], seq_count) + slots * seq_count
    send_index = (frame_local * frame_max + row_of).reshape(-1)
    outgoing = visual_frames.reshape(frames_dev * frame_max, d_cols)[send_index]
    received = lax.all_to_all(outgoing, "seq", split_axis=0, concat_axis=0, tiled=True)
    query_pos = jnp.arange(tok_rows, dtype=jnp.int32) * seq_count + seq_index
    before = ends[None, :] <= query_pos[:, None]
    frame = jnp.sum(before.astype(jnp.int32), axis=1)
    offset = jnp.sum(jnp.where(before, frame_tokens[None, :], 0), axis=1)
    slot_index = frame * cap_frame + (query_pos - offset) // seq_count
    visual = received[slot_index]
    wide = head_weights.reshape(d_cols, KV_HEADS, GROUP_HEADS + 2, HEAD_DIM)
    query_w = wide[:, :, :GROUP_HEADS].reshape(d_cols, KV_HEADS * rep_count, heads_local * HEAD_DIM)
    pair_w = wide[:, :, GROUP_HEADS:].reshape(d_cols, KV_HEADS, 2 * HEAD_DIM)
    pair_part = jnp.einsum("tc,cgw->gtw", visual, pair_w, preferred_element_type=jnp.float32)
    pair_part = jnp.broadcast_to(
        pair_part[:, None], (KV_HEADS, rep_count) + pair_part.shape[1:]
    ).reshape((KV_HEADS * rep_count,) + pair_part.shape[1:])
    pair_own = lax.psum_scatter(
        pair_part, ("kvh", "rep"), scatter_dimension=0, tiled=True
    )[0].astype(jnp.bfloat16)
    query_part = jnp.einsum("tc,cpw->ptw", visual, query_w, preferred_element_type=jnp.float32)
    queries = ring_reduce_scatter(query_part).astype(jnp.bfloat16)
    queries = queries.reshape(tok_rows, heads_local, HEAD_DIM)
    pair_all = lax.all_gather(pair_own, "seq", axis=0, tiled=False)
    return causal_attention(seq_index, queries, pair_all)


def solution(mesh):
    placed = (P("seq", "kvh", None), P(), P(), P(None, ("kvh", "rep")), P(("kvh", "rep"), None))
    return jax.shard_map(
        local, mesh=mesh, in_specs=placed, out_specs=P(None, "seq", ("kvh", "rep")), check_vma=False
    )
```

```python
import functools

import jax
import jax.numpy as jnp
from jax import lax
from jax.experimental import pallas as pl
from jax.experimental.pallas import tpu as pltpu
from jax.sharding import PartitionSpec as P

KV_HEADS = 4
HEAD_DIM = 128
GROUP_HEADS = 4


norm_eps = 1e-06
masked_score = -1e30
UNROLL = 8


def layer_norm(states, norm_gain):
    values = states.astype(jnp.float32)
    center = values - jnp.mean(values, axis=-1, keepdims=True)
    spread = jnp.mean(center * center, axis=-1, keepdims=True)
    return (center * lax.rsqrt(spread + norm_eps) * norm_gain).astype(jnp.bfloat16)


def attention_kernel(seq_ref, q_ref, kv_ref, o_ref, *, shards, tok_rows, block):
    seq_index = seq_ref[0]
    scale = HEAD_DIM ** (-0.5)
    rows = q_ref.shape[0] // (tok_rows // block)
    for qb in range(tok_rows // block):
        width = (((qb + 1) * block - 1) // 128 + 1) * 128
        q = q_ref[qb * rows : (qb + 1) * rows, :]
        row_j = qb * block + lax.broadcasted_iota(jnp.int32, (rows, 1), 0) % block
        query_pos = row_j * shards + seq_index
        lane_pos = lax.broadcasted_iota(jnp.int32, (1, width), 1) * shards

        def body(src, carry):
            top, total, context = carry
            first = pl.multiple_of(src * tok_rows, tok_rows)
            key = kv_ref[pl.ds(first, width), :HEAD_DIM]
            value = kv_ref[pl.ds(first, width), HEAD_DIM:]
            scores = lax.dot_general(
                q, key, (((1,), (1,)), ((), ())), preferred_element_type=jnp.float32
            ) * scale
            allowed = lane_pos <= query_pos - src
            scores = jnp.where(allowed, scores, masked_score)
            new_top = jnp.maximum(top, jnp.max(scores, axis=1, keepdims=True))
            shrink = jnp.exp(top - new_top)
            weights = jnp.exp(scores - new_top)
            total = shrink * total + jnp.sum(weights, axis=1, keepdims=True)
            update = jnp.dot(
                weights.astype(jnp.bfloat16), value, preferred_element_type=jnp.float32
            )
            return new_top, total, shrink * context + update

        start = (
            jnp.full((rows, 1), masked_score, jnp.float32),
            jnp.zeros((rows, 1), jnp.float32),
            jnp.zeros((rows, HEAD_DIM), jnp.float32),
        )
        top, total, context = lax.fori_loop(0, shards, body, start, unroll=UNROLL)
        o_ref[qb * rows : (qb + 1) * rows, :] = (context / total).astype(o_ref.dtype)


def causal_attention(seq_index, queries, pair_all, block=128):
    tok_rows, heads_local, _ = queries.shape
    shards = pair_all.shape[0]
    blocks = tok_rows // block
    q_rows = (
        queries.reshape(blocks, block, heads_local, HEAD_DIM)
        .transpose(0, 2, 1, 3)
        .reshape(tok_rows * heads_local, HEAD_DIM)
    )
    kv_rows = pair_all.reshape(shards * tok_rows, 2 * HEAD_DIM)
    out = pl.pallas_call(
        functools.partial(attention_kernel, shards=shards, tok_rows=tok_rows, block=block),
        out_shape=jax.ShapeDtypeStruct((tok_rows * heads_local, HEAD_DIM), jnp.bfloat16),
        in_specs=[
            pl.BlockSpec(memory_space=pltpu.SMEM),
            pl.BlockSpec(memory_space=pltpu.VMEM),
            pl.BlockSpec(memory_space=pltpu.VMEM),
        ],
        out_specs=pl.BlockSpec(memory_space=pltpu.VMEM),
        compiler_params=pltpu.CompilerParams(vmem_limit_bytes=48 * 1024 * 1024),
        cost_estimate=pl.CostEstimate(
            flops=4 * tok_rows * heads_local * shards * tok_rows * HEAD_DIM * 3 // 4,
            transcendentals=tok_rows * heads_local * shards * tok_rows * 3 // 4,
            bytes_accessed=kv_rows.size * 2 + 2 * q_rows.size * 2,
        ),
    )(jnp.reshape(seq_index, (1,)).astype(jnp.int32), q_rows, kv_rows)
    return (
        out.reshape(blocks, heads_local, block, HEAD_DIM)
        .transpose(0, 2, 1, 3)
        .reshape(tok_rows, 1, heads_local * HEAD_DIM)
    )


def ring_reduce_scatter(parts):
    count = parts.shape[0]
    axes = ("kvh", "rep")
    index = lax.axis_index("kvh") * lax.axis_size("rep") + lax.axis_index("rep")
    half = parts.shape[-1] // 2
    sums = []
    for step_dir, piece in ((1, parts[..., :half]), (-1, parts[..., half:])):
        perm = [(i, (i + step_dir) % count) for i in range(count)]
        buf = lax.dynamic_index_in_dim(piece, (index - step_dir) % count, 0, keepdims=False)
        for t in range(1, count):
            buf = lax.ppermute(buf, axes, perm)
            own = lax.dynamic_index_in_dim(piece, (index - step_dir * (t + 1)) % count, 0, keepdims=False)
            buf = buf + own
        sums.append(buf)
    return jnp.concatenate(sums, axis=-1)


def local(vision_states, frame_tokens, norm_gain, projector, head_weights):
    seq_count = lax.axis_size("seq")
    seq_index = lax.axis_index("seq")
    rep_count = lax.axis_size("rep")
    frames_dev = vision_states.shape[0]
    frame_max = vision_states.shape[1] * lax.axis_size("kvh")
    d_cols = projector.shape[1]
    cap_frame = frame_max // seq_count
    tok_rows = 2 * frames_dev * frame_max // 3
    heads_local = GROUP_HEADS // rep_count
    normed = layer_norm(vision_states, norm_gain)
    frame_rows = lax.all_gather(normed[0], "kvh", axis=0, tiled=False).reshape(1, frame_max, -1)
    hidden = jnp.einsum(
        "frv,vc->frc",
        frame_rows,
        projector,
        preferred_element_type=jnp.float32,
    )
    visual_frames = jax.nn.gelu(hidden, approximate=False).astype(jnp.bfloat16)
    ends = jnp.cumsum(frame_tokens)
    starts_all = ends - frame_tokens
    my_starts = lax.dynamic_slice_in_dim(starts_all, seq_index * frames_dev, frames_dev, 0)
    dest = jnp.arange(seq_count, dtype=jnp.int32)[:, None, None]
    slots = jnp.arange(cap_frame, dtype=jnp.int32)[None, None, :]
    frame_local = jnp.arange(frames_dev, dtype=jnp.int32)[None, :, None]
    row_of = jnp.mod(dest - my_starts[None, :, None], seq_count) + slots * seq_count
    send_index = (frame_local * frame_max + row_of).reshape(-1)
    outgoing = visual_frames.reshape(frames_dev * frame_max, d_cols)[send_index]
    received = lax.all_to_all(outgoing, "seq", split_axis=0, concat_axis=0, tiled=True)
    query_pos = jnp.arange(tok_rows, dtype=jnp.int32) * seq_count + seq_index
    before = ends[None, :] <= query_pos[:, None]
    frame = jnp.sum(before.astype(jnp.int32), axis=1)
    offset = jnp.sum(jnp.where(before, frame_tokens[None, :], 0), axis=1)
    slot_index = frame * cap_frame + (query_pos - offset) // seq_count
    visual = received[slot_index]
    wide = head_weights.reshape(d_cols, KV_HEADS, GROUP_HEADS + 2, HEAD_DIM)
    query_w = wide[:, :, :GROUP_HEADS].reshape(d_cols, KV_HEADS * rep_count, heads_local * HEAD_DIM)
    pair_w = wide[:, :, GROUP_HEADS:].reshape(d_cols, KV_HEADS, 2 * HEAD_DIM)
    pair_part = jnp.einsum("tc,cgw->gtw", visual, pair_w, preferred_element_type=jnp.float32)
    pair_part = jnp.broadcast_to(
        pair_part[:, None], (KV_HEADS, rep_count) + pair_part.shape[1:]
    ).reshape((KV_HEADS * rep_count,) + pair_part.shape[1:])
    pair_own = lax.psum_scatter(
        pair_part, ("kvh", "rep"), scatter_dimension=0, tiled=True
    )[0].astype(jnp.bfloat16)
    query_part = jnp.einsum("tc,cpw->ptw", visual, query_w, preferred_element_type=jnp.float32)
    queries = ring_reduce_scatter(query_part).astype(jnp.bfloat16)
    queries = queries.reshape(tok_rows, heads_local, HEAD_DIM)
    pair_all = lax.all_gather(pair_own, "seq", axis=0, tiled=False)
    return causal_attention(seq_index, queries, pair_all)


def solution(mesh):
    placed = (P("seq", "kvh", None), P(), P(), P(None, ("kvh", "rep")), P(("kvh", "rep"), None))
    return jax.shard_map(
        local, mesh=mesh, in_specs=placed, out_specs=P(None, "seq", ("kvh", "rep")), check_vma=False
    )
```

```python
import functools

import jax
import jax.numpy as jnp
from jax import lax
from jax.experimental import pallas as pl
from jax.experimental.pallas import tpu as pltpu
from jax.sharding import PartitionSpec as P

KV_HEADS = 4
HEAD_DIM = 128
GROUP_HEADS = 4


norm_eps = 1e-06
masked_score = -1e30
UNROLL = 8


def layer_norm(states, norm_gain):
    values = states.astype(jnp.float32)
    center = values - jnp.mean(values, axis=-1, keepdims=True)
    spread = jnp.mean(center * center, axis=-1, keepdims=True)
    return (center * lax.rsqrt(spread + norm_eps) * norm_gain).astype(jnp.bfloat16)


def attention_kernel(seq_ref, q_ref, kv_ref, o_ref, *, shards, tok_rows, block):
    seq_index = seq_ref[0]
    scale = HEAD_DIM ** (-0.5)
    blocks = tok_rows // block
    rows = q_ref.shape[0] // blocks
    setups = []
    for qb in range(blocks):
        width = (((qb + 1) * block - 1) // 128 + 1) * 128
        row_j = qb * block + lax.broadcasted_iota(jnp.int32, (rows, 1), 0) % block
        lane_pos = lax.broadcasted_iota(jnp.int32, (1, width), 1) * shards
        setups.append((width, row_j * shards + seq_index, lane_pos))

    def body(src, carry):
        first = pl.multiple_of(src * tok_rows, tok_rows)
        out = []
        for qb in range(blocks):
            width, query_pos, lane_pos = setups[qb]
            top, total, context = carry[qb]
            q = q_ref[qb * rows : (qb + 1) * rows, :]
            key = kv_ref[pl.ds(first, width), :HEAD_DIM]
            value = kv_ref[pl.ds(first, width), HEAD_DIM:]
            scores = lax.dot_general(
                q, key, (((1,), (1,)), ((), ())), preferred_element_type=jnp.float32
            ) * scale
            allowed = lane_pos <= query_pos - src
            scores = jnp.where(allowed, scores, masked_score)
            new_top = jnp.maximum(top, jnp.max(scores, axis=1, keepdims=True))
            shrink = jnp.exp(top - new_top)
            weights = jnp.exp(scores - new_top)
            total = shrink * total + jnp.sum(weights, axis=1, keepdims=True)
            update = jnp.dot(
                weights.astype(jnp.bfloat16), value, preferred_element_type=jnp.float32
            )
            out.append((new_top, total, shrink * context + update))
        return tuple(out)

    start = tuple(
        (
            jnp.full((rows, 1), masked_score, jnp.float32),
            jnp.zeros((rows, 1), jnp.float32),
            jnp.zeros((rows, HEAD_DIM), jnp.float32),
        )
        for _ in range(blocks)
    )
    final = lax.fori_loop(0, shards, body, start, unroll=UNROLL)
    for qb in range(blocks):
        _, total, context = final[qb]
        o_ref[qb * rows : (qb + 1) * rows, :] = (context / total).astype(o_ref.dtype)


def causal_attention(seq_index, queries, pair_all, block=128):
    tok_rows, heads_local, _ = queries.shape
    shards = pair_all.shape[0]
    blocks = tok_rows // block
    q_rows = (
        queries.reshape(blocks, block, heads_local, HEAD_DIM)
        .transpose(0, 2, 1, 3)
        .reshape(tok_rows * heads_local, HEAD_DIM)
    )
    kv_rows = pair_all.reshape(shards * tok_rows, 2 * HEAD_DIM)
    out = pl.pallas_call(
        functools.partial(attention_kernel, shards=shards, tok_rows=tok_rows, block=block),
        out_shape=jax.ShapeDtypeStruct((tok_rows * heads_local, HEAD_DIM), jnp.bfloat16),
        in_specs=[
            pl.BlockSpec(memory_space=pltpu.SMEM),
            pl.BlockSpec(memory_space=pltpu.VMEM),
            pl.BlockSpec(memory_space=pltpu.VMEM),
        ],
        out_specs=pl.BlockSpec(memory_space=pltpu.VMEM),
        compiler_params=pltpu.CompilerParams(vmem_limit_bytes=48 * 1024 * 1024),
        cost_estimate=pl.CostEstimate(
            flops=4 * tok_rows * heads_local * shards * tok_rows * HEAD_DIM * 3 // 4,
            transcendentals=tok_rows * heads_local * shards * tok_rows * 3 // 4,
            bytes_accessed=kv_rows.size * 2 + 2 * q_rows.size * 2,
        ),
    )(jnp.reshape(seq_index, (1,)).astype(jnp.int32), q_rows, kv_rows)
    return (
        out.reshape(blocks, heads_local, block, HEAD_DIM)
        .transpose(0, 2, 1, 3)
        .reshape(tok_rows, 1, heads_local * HEAD_DIM)
    )


def ring_all_gather(block, axis):
    count = lax.axis_size(axis)
    forward = [(i, (i + 1) % count) for i in range(count)]
    backward = [(i, (i - 1) % count) for i in range(count)]
    placed = {0: block}
    ahead, behind = block, block
    for step in range(1, (count - 1) // 2 + 1):
        behind = lax.ppermute(behind, axis, forward)
        ahead = lax.ppermute(ahead, axis, backward)
        placed[count - step] = behind
        placed[step] = ahead
    if count % 2 == 0 and count > 1:
        placed[count // 2] = lax.ppermute(behind, axis, forward)
    return jnp.stack([placed[k] for k in range(count)])


def ring_reduce_scatter(parts):
    count = parts.shape[0]
    axes = ("kvh", "rep")
    index = lax.axis_index("kvh") * lax.axis_size("rep") + lax.axis_index("rep")
    half = parts.shape[-1] // 2
    sums = []
    for step_dir, piece in ((1, parts[..., :half]), (-1, parts[..., half:])):
        perm = [(i, (i + step_dir) % count) for i in range(count)]
        buf = lax.dynamic_index_in_dim(piece, (index - step_dir) % count, 0, keepdims=False)
        for t in range(1, count):
            buf = lax.ppermute(buf, axes, perm)
            own = lax.dynamic_index_in_dim(piece, (index - step_dir * (t + 1)) % count, 0, keepdims=False)
            buf = buf + own
        sums.append(buf)
    return jnp.concatenate(sums, axis=-1)


def local(vision_states, frame_tokens, norm_gain, projector, head_weights):
    seq_count = lax.axis_size("seq")
    seq_index = lax.axis_index("seq")
    rep_count = lax.axis_size("rep")
    frames_dev = vision_states.shape[0]
    frame_max = vision_states.shape[1] * lax.axis_size("kvh")
    d_cols = projector.shape[1]
    cap_frame = frame_max // seq_count
    tok_rows = 2 * frames_dev * frame_max // 3
    heads_local = GROUP_HEADS // rep_count
    normed = layer_norm(vision_states, norm_gain)
    kvh_index = lax.axis_index("kvh")
    rows_dev = vision_states.shape[1]
    frame_rows = ring_all_gather(normed[0], "kvh").reshape(1, frame_max, -1)
    hidden = jnp.einsum(
        "frv,vc->frc",
        frame_rows,
        projector,
        preferred_element_type=jnp.float32,
    )
    visual_frames = jax.nn.gelu(hidden, approximate=False).astype(jnp.bfloat16)
    ends = jnp.cumsum(frame_tokens)
    starts_all = ends - frame_tokens
    my_starts = lax.dynamic_slice_in_dim(starts_all, seq_index * frames_dev, frames_dev, 0)
    dest = jnp.arange(seq_count, dtype=jnp.int32)[:, None, None]
    slots = jnp.arange(cap_frame, dtype=jnp.int32)[None, None, :]
    frame_local = jnp.arange(frames_dev, dtype=jnp.int32)[None, :, None]
    row_of = jnp.mod(dest - my_starts[None, :, None], seq_count) + slots * seq_count
    row_of = jnp.mod(row_of // rows_dev - kvh_index, lax.axis_size("kvh")) * rows_dev + row_of % rows_dev
    send_index = (frame_local * frame_max + row_of).reshape(-1)
    outgoing = visual_frames.reshape(frames_dev * frame_max, d_cols)[send_index]
    received = lax.all_to_all(outgoing, "seq", split_axis=0, concat_axis=0, tiled=True)
    query_pos = jnp.arange(tok_rows, dtype=jnp.int32) * seq_count + seq_index
    before = ends[None, :] <= query_pos[:, None]
    frame = jnp.sum(before.astype(jnp.int32), axis=1)
    offset = jnp.sum(jnp.where(before, frame_tokens[None, :], 0), axis=1)
    slot_index = frame * cap_frame + (query_pos - offset) // seq_count
    visual = received[slot_index]
    wide = head_weights.reshape(d_cols, KV_HEADS, GROUP_HEADS + 2, HEAD_DIM)
    query_w = wide[:, :, :GROUP_HEADS].reshape(d_cols, KV_HEADS * rep_count, heads_local * HEAD_DIM)
    pair_w = wide[:, :, GROUP_HEADS:].reshape(d_cols, KV_HEADS, 2 * HEAD_DIM)
    pair_part = jnp.einsum("tc,cgw->gtw", visual, pair_w, preferred_element_type=jnp.float32)
    pair_part = jnp.broadcast_to(
        pair_part[:, None], (KV_HEADS, rep_count) + pair_part.shape[1:]
    ).reshape((KV_HEADS * rep_count,) + pair_part.shape[1:])
    pair_own = lax.psum_scatter(
        pair_part, ("kvh", "rep"), scatter_dimension=0, tiled=True
    )[0].astype(jnp.bfloat16)
    query_part = jnp.einsum("tc,cpw->ptw", visual, query_w, preferred_element_type=jnp.float32)
    queries = ring_reduce_scatter(query_part).astype(jnp.bfloat16)
    queries = queries.reshape(tok_rows, heads_local, HEAD_DIM)
    pair_all = lax.all_gather(pair_own, "seq", axis=0, tiled=False)
    return causal_attention(seq_index, queries, pair_all)


def solution(mesh):
    placed = (P("seq", "kvh", None), P(), P(), P(None, ("kvh", "rep")), P(("kvh", "rep"), None))
    return jax.shard_map(
        local, mesh=mesh, in_specs=placed, out_specs=P(None, "seq", ("kvh", "rep")), check_vma=False
    )
```

```python
import functools

import jax
import jax.numpy as jnp
from jax import lax
from jax.experimental import pallas as pl
from jax.experimental.pallas import tpu as pltpu
from jax.sharding import PartitionSpec as P

KV_HEADS = 4
HEAD_DIM = 128
GROUP_HEADS = 4


norm_eps = 1e-06
masked_score = -1e30
UNROLL = 8


def layer_norm(states, norm_gain):
    values = states.astype(jnp.float32)
    center = values - jnp.mean(values, axis=-1, keepdims=True)
    spread = jnp.mean(center * center, axis=-1, keepdims=True)
    return (center * lax.rsqrt(spread + norm_eps) * norm_gain).astype(jnp.bfloat16)


def attention_kernel(seq_ref, q_ref, kv_ref, o_ref, *, shards, tok_rows, block):
    seq_index = seq_ref[0]
    scale = HEAD_DIM ** (-0.5)
    blocks = tok_rows // block
    rows = q_ref.shape[0] // blocks
    setups = []
    for qb in range(blocks):
        width = (((qb + 1) * block - 1) // 128 + 1) * 128
        row_j = qb * block + lax.broadcasted_iota(jnp.int32, (rows, 1), 0) % block
        lane_pos = lax.broadcasted_iota(jnp.int32, (1, width), 1) * shards
        setups.append((width, row_j * shards + seq_index, lane_pos))

    def body(src, carry):
        first = pl.multiple_of(src * tok_rows, tok_rows)
        out = []
        for qb in range(blocks):
            width, query_pos, lane_pos = setups[qb]
            top, total, context = carry[qb]
            q = q_ref[qb * rows : (qb + 1) * rows, :]
            key = kv_ref[pl.ds(first, width), :HEAD_DIM]
            value = kv_ref[pl.ds(first, width), HEAD_DIM:]
            scores = lax.dot_general(
                q, key, (((1,), (1,)), ((), ())), preferred_element_type=jnp.float32
            ) * scale
            allowed = lane_pos <= query_pos - src
            scores = jnp.where(allowed, scores, masked_score)
            new_top = jnp.maximum(top, jnp.max(scores, axis=1, keepdims=True))
            shrink = jnp.exp(top - new_top)
            weights = jnp.exp(scores - new_top)
            total = shrink * total + jnp.sum(weights, axis=1, keepdims=True)
            update = jnp.dot(
                weights.astype(jnp.bfloat16), value, preferred_element_type=jnp.float32
            )
            out.append((new_top, total, shrink * context + update))
        return tuple(out)

    start = tuple(
        (
            jnp.full((rows, 1), masked_score, jnp.float32),
            jnp.zeros((rows, 1), jnp.float32),
            jnp.zeros((rows, HEAD_DIM), jnp.float32),
        )
        for _ in range(blocks)
    )
    final = lax.fori_loop(0, shards, body, start, unroll=UNROLL)
    for qb in range(blocks):
        _, total, context = final[qb]
        o_ref[qb * rows : (qb + 1) * rows, :] = (context / total).astype(o_ref.dtype)


def causal_attention(seq_index, queries, pair_all, block=128):
    tok_rows, heads_local, _ = queries.shape
    shards = pair_all.shape[0]
    blocks = tok_rows // block
    q_rows = (
        queries.reshape(blocks, block, heads_local, HEAD_DIM)
        .transpose(0, 2, 1, 3)
        .reshape(tok_rows * heads_local, HEAD_DIM)
    )
    kv_rows = pair_all.reshape(shards * tok_rows, 2 * HEAD_DIM)
    out = pl.pallas_call(
        functools.partial(attention_kernel, shards=shards, tok_rows=tok_rows, block=block),
        out_shape=jax.ShapeDtypeStruct((tok_rows * heads_local, HEAD_DIM), jnp.bfloat16),
        in_specs=[
            pl.BlockSpec(memory_space=pltpu.SMEM),
            pl.BlockSpec(memory_space=pltpu.VMEM),
            pl.BlockSpec(memory_space=pltpu.VMEM),
        ],
        out_specs=pl.BlockSpec(memory_space=pltpu.VMEM),
        compiler_params=pltpu.CompilerParams(vmem_limit_bytes=48 * 1024 * 1024),
        cost_estimate=pl.CostEstimate(
            flops=4 * tok_rows * heads_local * shards * tok_rows * HEAD_DIM * 3 // 4,
            transcendentals=tok_rows * heads_local * shards * tok_rows * 3 // 4,
            bytes_accessed=kv_rows.size * 2 + 2 * q_rows.size * 2,
        ),
    )(jnp.reshape(seq_index, (1,)).astype(jnp.int32), q_rows, kv_rows)
    return (
        out.reshape(blocks, heads_local, block, HEAD_DIM)
        .transpose(0, 2, 1, 3)
        .reshape(tok_rows, 1, heads_local * HEAD_DIM)
    )


def ring_reduce_scatter(parts):
    count = parts.shape[0]
    axes = ("kvh", "rep")
    index = lax.axis_index("kvh") * lax.axis_size("rep") + lax.axis_index("rep")
    half = parts.shape[-1] // 2
    sums = []
    for step_dir, piece in ((1, parts[..., :half]), (-1, parts[..., half:])):
        perm = [(i, (i + step_dir) % count) for i in range(count)]
        buf = lax.dynamic_index_in_dim(piece, (index - step_dir) % count, 0, keepdims=False)
        for t in range(1, count):
            buf = lax.ppermute(buf, axes, perm)
            own = lax.dynamic_index_in_dim(piece, (index - step_dir * (t + 1)) % count, 0, keepdims=False)
            buf = buf + own
        sums.append(buf)
    return jnp.concatenate(sums, axis=-1)


def local(vision_states, frame_tokens, norm_gain, projector, head_weights):
    seq_count = lax.axis_size("seq")
    seq_index = lax.axis_index("seq")
    rep_count = lax.axis_size("rep")
    frames_dev = vision_states.shape[0]
    frame_max = vision_states.shape[1] * lax.axis_size("kvh")
    d_cols = projector.shape[1]
    cap_frame = frame_max // seq_count
    tok_rows = 2 * frames_dev * frame_max // 3
    heads_local = GROUP_HEADS // rep_count
    normed = layer_norm(vision_states, norm_gain)
    frame_rows = lax.all_gather(normed[0], "kvh", axis=0, tiled=False).reshape(1, frame_max, -1)
    hidden = jnp.einsum(
        "frv,vc->frc",
        frame_rows,
        projector,
        preferred_element_type=jnp.float32,
    )
    visual_frames = jax.nn.gelu(hidden, approximate=False).astype(jnp.bfloat16)
    ends = jnp.cumsum(frame_tokens)
    starts_all = ends - frame_tokens
    my_starts = lax.dynamic_slice_in_dim(starts_all, seq_index * frames_dev, frames_dev, 0)
    dest = jnp.arange(seq_count, dtype=jnp.int32)[:, None, None]
    slots = jnp.arange(cap_frame, dtype=jnp.int32)[None, None, :]
    frame_local = jnp.arange(frames_dev, dtype=jnp.int32)[None, :, None]
    row_of = jnp.mod(dest - my_starts[None, :, None], seq_count) + slots * seq_count
    send_index = (frame_local * frame_max + row_of).reshape(-1)
    outgoing = visual_frames.reshape(frames_dev * frame_max, d_cols)[send_index]
    received = lax.all_to_all(outgoing, "seq", split_axis=0, concat_axis=0, tiled=True)
    query_pos = jnp.arange(tok_rows, dtype=jnp.int32) * seq_count + seq_index
    before = ends[None, :] <= query_pos[:, None]
    frame = jnp.sum(before.astype(jnp.int32), axis=1)
    offset = jnp.sum(jnp.where(before, frame_tokens[None, :], 0), axis=1)
    slot_index = frame * cap_frame + (query_pos - offset) // seq_count
    visual = received[slot_index]
    wide = head_weights.reshape(d_cols, KV_HEADS, GROUP_HEADS + 2, HEAD_DIM)
    query_w = wide[:, :, :GROUP_HEADS].reshape(d_cols, KV_HEADS * rep_count, heads_local * HEAD_DIM)
    pair_w = wide[:, :, GROUP_HEADS:].reshape(d_cols, KV_HEADS, 2 * HEAD_DIM)
    pair_part = jnp.einsum("tc,cgw->gtw", visual, pair_w, preferred_element_type=jnp.float32)
    pair_part = jnp.broadcast_to(
        pair_part[:, None], (KV_HEADS, rep_count) + pair_part.shape[1:]
    ).reshape((KV_HEADS * rep_count,) + pair_part.shape[1:])
    pair_own = lax.psum_scatter(
        pair_part, ("kvh", "rep"), scatter_dimension=0, tiled=True
    )[0].astype(jnp.bfloat16)
    query_part = jnp.einsum("tc,cpw->ptw", visual, query_w, preferred_element_type=jnp.float32)
    queries = ring_reduce_scatter(query_part).astype(jnp.bfloat16)
    queries = queries.reshape(tok_rows, heads_local, HEAD_DIM)
    pair_all = lax.all_gather(pair_own, "seq", axis=0, tiled=False)
    return causal_attention(seq_index, queries, pair_all)


def solution(mesh):
    placed = (P("seq", "kvh", None), P(), P(), P(None, ("kvh", "rep")), P(("kvh", "rep"), None))
    return jax.shard_map(
        local, mesh=mesh, in_specs=placed, out_specs=P(None, "seq", ("kvh", "rep")), check_vma=False
    )
```

```python
import functools

import jax
import jax.numpy as jnp
from jax import lax
from jax.experimental import pallas as pl
from jax.experimental.pallas import tpu as pltpu
from jax.sharding import PartitionSpec as P

KV_HEADS = 4
HEAD_DIM = 128
GROUP_HEADS = 4


norm_eps = 1e-06
masked_score = -1e30
UNROLL = 8


def layer_norm(states, norm_gain):
    values = states.astype(jnp.float32)
    center = values - jnp.mean(values, axis=-1, keepdims=True)
    spread = jnp.mean(center * center, axis=-1, keepdims=True)
    return (center * lax.rsqrt(spread + norm_eps) * norm_gain).astype(jnp.bfloat16)


def attention_kernel(seq_ref, q_ref, kv_ref, o_ref, *, shards, tok_rows, block):
    seq_index = seq_ref[0]
    scale = HEAD_DIM ** (-0.5)
    blocks = tok_rows // block
    rows = q_ref.shape[0] // blocks
    setups = []
    for qb in range(blocks):
        width = (((qb + 1) * block - 1) // 128 + 1) * 128
        row_j = qb * block + lax.broadcasted_iota(jnp.int32, (rows, 1), 0) % block
        lane_pos = lax.broadcasted_iota(jnp.int32, (1, width), 1) * shards
        setups.append((width, row_j * shards + seq_index, lane_pos))

    def body(src, carry):
        first = pl.multiple_of(src * tok_rows, tok_rows)
        out = []
        for qb in range(blocks):
            width, query_pos, lane_pos = setups[qb]
            top, total, context = carry[qb]
            q = q_ref[qb * rows : (qb + 1) * rows, :]
            key = kv_ref[pl.ds(first, width), :HEAD_DIM]
            value = kv_ref[pl.ds(first, width), HEAD_DIM:]
            scores = lax.dot_general(
                q, key, (((1,), (1,)), ((), ())), preferred_element_type=jnp.float32
            ) * scale
            allowed = lane_pos <= query_pos - src
            scores = jnp.where(allowed, scores, masked_score)
            new_top = jnp.maximum(top, jnp.max(scores, axis=1, keepdims=True))
            shrink = jnp.exp(top - new_top)
            weights = jnp.exp(scores - new_top)
            total = shrink * total + jnp.sum(weights, axis=1, keepdims=True)
            update = jnp.dot(
                weights.astype(jnp.bfloat16), value, preferred_element_type=jnp.float32
            )
            out.append((new_top, total, shrink * context + update))
        return tuple(out)

    start = tuple(
        (
            jnp.full((rows, 1), masked_score, jnp.float32),
            jnp.zeros((rows, 1), jnp.float32),
            jnp.zeros((rows, HEAD_DIM), jnp.float32),
        )
        for _ in range(blocks)
    )
    final = lax.fori_loop(0, shards, body, start, unroll=UNROLL)
    for qb in range(blocks):
        _, total, context = final[qb]
        o_ref[qb * rows : (qb + 1) * rows, :] = (context / total).astype(o_ref.dtype)


def causal_attention(seq_index, queries, pair_all, block=128):
    tok_rows, heads_local, _ = queries.shape
    shards = pair_all.shape[0]
    blocks = tok_rows // block
    q_rows = (
        queries.reshape(blocks, block, heads_local, HEAD_DIM)
        .transpose(0, 2, 1, 3)
        .reshape(tok_rows * heads_local, HEAD_DIM)
    )
    kv_rows = pair_all.reshape(shards * tok_rows, 2 * HEAD_DIM)
    out = pl.pallas_call(
        functools.partial(attention_kernel, shards=shards, tok_rows=tok_rows, block=block),
        out_shape=jax.ShapeDtypeStruct((tok_rows * heads_local, HEAD_DIM), jnp.bfloat16),
        in_specs=[
            pl.BlockSpec(memory_space=pltpu.SMEM),
            pl.BlockSpec(memory_space=pltpu.VMEM),
            pl.BlockSpec(memory_space=pltpu.VMEM),
        ],
        out_specs=pl.BlockSpec(memory_space=pltpu.VMEM),
        compiler_params=pltpu.CompilerParams(vmem_limit_bytes=48 * 1024 * 1024),
        cost_estimate=pl.CostEstimate(
            flops=4 * tok_rows * heads_local * shards * tok_rows * HEAD_DIM * 3 // 4,
            transcendentals=tok_rows * heads_local * shards * tok_rows * 3 // 4,
            bytes_accessed=kv_rows.size * 2 + 2 * q_rows.size * 2,
        ),
    )(jnp.reshape(seq_index, (1,)).astype(jnp.int32), q_rows, kv_rows)
    return (
        out.reshape(blocks, heads_local, block, HEAD_DIM)
        .transpose(0, 2, 1, 3)
        .reshape(tok_rows, 1, heads_local * HEAD_DIM)
    )


def ring_reduce_scatter(parts):
    count = parts.shape[0]
    axes = ("kvh", "rep")
    index = lax.axis_index("kvh") * lax.axis_size("rep") + lax.axis_index("rep")
    half = parts.shape[-1] // 2
    sums = []
    for step_dir, piece in ((1, parts[..., :half]), (-1, parts[..., half:])):
        perm = [(i, (i + step_dir) % count) for i in range(count)]
        buf = lax.dynamic_index_in_dim(piece, (index - step_dir) % count, 0, keepdims=False)
        for t in range(1, count):
            buf = lax.ppermute(buf, axes, perm)
            own = lax.dynamic_index_in_dim(piece, (index - step_dir * (t + 1)) % count, 0, keepdims=False)
            buf = buf + own
        sums.append(buf)
    return jnp.concatenate(sums, axis=-1)


def local(vision_states, frame_tokens, norm_gain, projector, head_weights):
    seq_count = lax.axis_size("seq")
    seq_index = lax.axis_index("seq")
    rep_count = lax.axis_size("rep")
    frames_dev = vision_states.shape[0]
    frame_max = vision_states.shape[1] * lax.axis_size("kvh")
    d_cols = projector.shape[1]
    cap_frame = frame_max // seq_count
    tok_rows = 2 * frames_dev * frame_max // 3
    heads_local = GROUP_HEADS // rep_count
    normed = layer_norm(vision_states, norm_gain)
    frame_rows = lax.all_gather(normed[0], "kvh", axis=0, tiled=False).reshape(1, frame_max, -1)
    hidden = jnp.einsum(
        "frv,vc->frc",
        frame_rows,
        projector,
        preferred_element_type=jnp.float32,
    )
    visual_frames = jax.nn.gelu(hidden, approximate=False).astype(jnp.bfloat16)
    ends = jnp.cumsum(frame_tokens)
    starts_all = ends - frame_tokens
    my_starts = lax.dynamic_slice_in_dim(starts_all, seq_index * frames_dev, frames_dev, 0)
    dest = jnp.arange(seq_count, dtype=jnp.int32)[:, None, None]
    slots = jnp.arange(cap_frame, dtype=jnp.int32)[None, None, :]
    frame_local = jnp.arange(frames_dev, dtype=jnp.int32)[None, :, None]
    row_of = jnp.mod(dest - my_starts[None, :, None], seq_count) + slots * seq_count
    send_index = (frame_local * frame_max + row_of).reshape(-1)
    outgoing = visual_frames.reshape(frames_dev * frame_max, d_cols)[send_index]
    received = lax.all_to_all(outgoing, "seq", split_axis=0, concat_axis=0, tiled=True)
    query_pos = jnp.arange(tok_rows, dtype=jnp.int32) * seq_count + seq_index
    before = ends[None, :] <= query_pos[:, None]
    frame = jnp.sum(before.astype(jnp.int32), axis=1)
    offset = jnp.sum(jnp.where(before, frame_tokens[None, :], 0), axis=1)
    slot_index = frame * cap_frame + (query_pos - offset) // seq_count
    visual = received[slot_index]
    wide = head_weights.reshape(d_cols, KV_HEADS, GROUP_HEADS + 2, HEAD_DIM)
    query_w = wide[:, :, :GROUP_HEADS].reshape(d_cols, KV_HEADS * rep_count, heads_local * HEAD_DIM)
    pair_w = wide[:, :, GROUP_HEADS:].reshape(d_cols, KV_HEADS, 2 * HEAD_DIM)
    pair_part = jnp.einsum("tc,cgw->gtw", visual, pair_w, preferred_element_type=jnp.float32)
    pair_part = jnp.broadcast_to(
        pair_part[:, None], (KV_HEADS, rep_count) + pair_part.shape[1:]
    ).reshape((KV_HEADS * rep_count,) + pair_part.shape[1:])
    pair_own = lax.psum_scatter(
        pair_part.astype(jnp.bfloat16), ("kvh", "rep"), scatter_dimension=0, tiled=True
    )[0]
    query_part = jnp.einsum("tc,cpw->ptw", visual, query_w, preferred_element_type=jnp.float32)
    queries = ring_reduce_scatter(query_part).astype(jnp.bfloat16)
    queries = queries.reshape(tok_rows, heads_local, HEAD_DIM)
    pair_all = lax.all_gather(pair_own, "seq", axis=0, tiled=False)
    return causal_attention(seq_index, queries, pair_all)


def solution(mesh):
    placed = (P("seq", "kvh", None), P(), P(), P(None, ("kvh", "rep")), P(("kvh", "rep"), None))
    return jax.shard_map(
        local, mesh=mesh, in_specs=placed, out_specs=P(None, "seq", ("kvh", "rep")), check_vma=False
    )
```

```python
import functools

import jax
import jax.numpy as jnp
from jax import lax
from jax.experimental import pallas as pl
from jax.experimental.pallas import tpu as pltpu
from jax.sharding import PartitionSpec as P

KV_HEADS = 4
HEAD_DIM = 128
GROUP_HEADS = 4


norm_eps = 1e-06
masked_score = -1e30
UNROLL = 8


def layer_norm(states, norm_gain):
    values = states.astype(jnp.float32)
    center = values - jnp.mean(values, axis=-1, keepdims=True)
    spread = jnp.mean(center * center, axis=-1, keepdims=True)
    return (center * lax.rsqrt(spread + norm_eps) * norm_gain).astype(jnp.bfloat16)


def attention_kernel(seq_ref, q_ref, kv_ref, o_ref, *, shards, tok_rows, block):
    seq_index = seq_ref[0]
    scale = HEAD_DIM ** (-0.5)
    blocks = tok_rows // block
    rows = q_ref.shape[0] // blocks
    setups = []
    for qb in range(blocks):
        width = (((qb + 1) * block - 1) // 128 + 1) * 128
        row_j = qb * block + lax.broadcasted_iota(jnp.int32, (rows, 1), 0) % block
        lane_pos = lax.broadcasted_iota(jnp.int32, (1, width), 1) * shards
        setups.append((width, row_j * shards + seq_index, lane_pos))

    def body(src, carry):
        first = pl.multiple_of(src * tok_rows, tok_rows)
        out = []
        for qb in range(blocks):
            width, query_pos, lane_pos = setups[qb]
            top, total, context = carry[qb]
            q = q_ref[qb * rows : (qb + 1) * rows, :]
            key = kv_ref[pl.ds(first, width), :HEAD_DIM]
            value = kv_ref[pl.ds(first, width), HEAD_DIM:]
            scores = lax.dot_general(
                q, key, (((1,), (1,)), ((), ())), preferred_element_type=jnp.float32
            ) * scale
            allowed = lane_pos <= query_pos - src
            scores = jnp.where(allowed, scores, masked_score)
            new_top = jnp.maximum(top, jnp.max(scores, axis=1, keepdims=True))
            shrink = jnp.exp(top - new_top)
            weights = jnp.exp(scores - new_top)
            total = shrink * total + jnp.sum(weights, axis=1, keepdims=True)
            update = jnp.dot(
                weights.astype(jnp.bfloat16), value, preferred_element_type=jnp.float32
            )
            out.append((new_top, total, shrink * context + update))
        return tuple(out)

    start = tuple(
        (
            jnp.full((rows, 1), masked_score, jnp.float32),
            jnp.zeros((rows, 1), jnp.float32),
            jnp.zeros((rows, HEAD_DIM), jnp.float32),
        )
        for _ in range(blocks)
    )
    final = lax.fori_loop(0, shards, body, start, unroll=UNROLL)
    for qb in range(blocks):
        _, total, context = final[qb]
        o_ref[qb * rows : (qb + 1) * rows, :] = (context / total).astype(o_ref.dtype)


def causal_attention(seq_index, queries, pair_all, block=128):
    tok_rows, heads_local, _ = queries.shape
    shards = pair_all.shape[0]
    blocks = tok_rows // block
    q_rows = (
        queries.reshape(blocks, block, heads_local, HEAD_DIM)
        .transpose(0, 2, 1, 3)
        .reshape(tok_rows * heads_local, HEAD_DIM)
    )
    kv_rows = pair_all.reshape(shards * tok_rows, 2 * HEAD_DIM)
    out = pl.pallas_call(
        functools.partial(attention_kernel, shards=shards, tok_rows=tok_rows, block=block),
        out_shape=jax.ShapeDtypeStruct((tok_rows * heads_local, HEAD_DIM), jnp.bfloat16),
        in_specs=[
            pl.BlockSpec(memory_space=pltpu.SMEM),
            pl.BlockSpec(memory_space=pltpu.VMEM),
            pl.BlockSpec(memory_space=pltpu.VMEM),
        ],
        out_specs=pl.BlockSpec(memory_space=pltpu.VMEM),
        compiler_params=pltpu.CompilerParams(vmem_limit_bytes=48 * 1024 * 1024),
        cost_estimate=pl.CostEstimate(
            flops=4 * tok_rows * heads_local * shards * tok_rows * HEAD_DIM * 3 // 4,
            transcendentals=tok_rows * heads_local * shards * tok_rows * 3 // 4,
            bytes_accessed=kv_rows.size * 2 + 2 * q_rows.size * 2,
        ),
    )(jnp.reshape(seq_index, (1,)).astype(jnp.int32), q_rows, kv_rows)
    return (
        out.reshape(blocks, heads_local, block, HEAD_DIM)
        .transpose(0, 2, 1, 3)
        .reshape(tok_rows, 1, heads_local * HEAD_DIM)
    )


def ring_reduce_scatter(parts):
    count = parts.shape[0]
    axes = ("kvh", "rep")
    index = lax.axis_index("kvh") * lax.axis_size("rep") + lax.axis_index("rep")
    half = parts.shape[-1] // 2
    sums = []
    for step_dir, piece in ((1, parts[..., :half]), (-1, parts[..., half:])):
        perm = [(i, (i + step_dir) % count) for i in range(count)]
        buf = lax.dynamic_index_in_dim(piece, (index - step_dir) % count, 0, keepdims=False)
        for t in range(1, count):
            buf = lax.ppermute(buf, axes, perm)
            own = lax.dynamic_index_in_dim(piece, (index - step_dir * (t + 1)) % count, 0, keepdims=False)
            buf = buf + own
        sums.append(buf)
    return jnp.concatenate(sums, axis=-1)


def local(vision_states, frame_tokens, norm_gain, projector, head_weights):
    seq_count = lax.axis_size("seq")
    seq_index = lax.axis_index("seq")
    rep_count = lax.axis_size("rep")
    frames_dev = vision_states.shape[0]
    frame_max = vision_states.shape[1] * lax.axis_size("kvh")
    d_cols = projector.shape[1]
    cap_frame = frame_max // seq_count
    tok_rows = 2 * frames_dev * frame_max // 3
    heads_local = GROUP_HEADS // rep_count
    normed = layer_norm(vision_states, norm_gain)
    frame_rows = lax.all_gather(normed[0], "kvh", axis=0, tiled=False).reshape(1, frame_max, -1)
    hidden = jnp.einsum(
        "frv,vc->frc",
        frame_rows,
        projector,
        preferred_element_type=jnp.float32,
    )
    visual_frames = jax.nn.gelu(hidden, approximate=False).astype(jnp.bfloat16)
    ends = jnp.cumsum(frame_tokens)
    starts_all = ends - frame_tokens
    my_starts = lax.dynamic_slice_in_dim(starts_all, seq_index * frames_dev, frames_dev, 0)
    dest = jnp.arange(seq_count, dtype=jnp.int32)[:, None, None]
    slots = jnp.arange(cap_frame, dtype=jnp.int32)[None, None, :]
    frame_local = jnp.arange(frames_dev, dtype=jnp.int32)[None, :, None]
    row_of = jnp.mod(dest - my_starts[None, :, None], seq_count) + slots * seq_count
    send_index = (frame_local * frame_max + row_of).reshape(-1)
    outgoing = visual_frames.reshape(frames_dev * frame_max, d_cols)[send_index]
    received = lax.all_to_all(outgoing, "seq", split_axis=0, concat_axis=0, tiled=True)
    query_pos = jnp.arange(tok_rows, dtype=jnp.int32) * seq_count + seq_index
    before = ends[None, :] <= query_pos[:, None]
    frame = jnp.sum(before.astype(jnp.int32), axis=1)
    offset = jnp.sum(jnp.where(before, frame_tokens[None, :], 0), axis=1)
    slot_index = frame * cap_frame + (query_pos - offset) // seq_count
    visual = received[slot_index]
    wide = head_weights.reshape(d_cols, KV_HEADS, GROUP_HEADS + 2, HEAD_DIM)
    query_w = wide[:, :, :GROUP_HEADS].reshape(d_cols, KV_HEADS * rep_count, heads_local * HEAD_DIM)
    pair_w = wide[:, :, GROUP_HEADS:].reshape(d_cols, KV_HEADS, 1, 2 * HEAD_DIM)
    pair_w = jnp.broadcast_to(pair_w, (d_cols, KV_HEADS, rep_count, 2 * HEAD_DIM)).reshape(
        d_cols, KV_HEADS * rep_count, 2 * HEAD_DIM
    )
    pair_part = jnp.einsum("tc,cpw->ptw", visual, pair_w, preferred_element_type=jnp.float32)
    pair_own = lax.psum_scatter(
        pair_part, ("kvh", "rep"), scatter_dimension=0, tiled=True
    )[0].astype(jnp.bfloat16)
    query_part = jnp.einsum("tc,cpw->ptw", visual, query_w, preferred_element_type=jnp.float32)
    queries = ring_reduce_scatter(query_part).astype(jnp.bfloat16)
    queries = queries.reshape(tok_rows, heads_local, HEAD_DIM)
    pair_all = lax.all_gather(pair_own, "seq", axis=0, tiled=False)
    return causal_attention(seq_index, queries, pair_all)


def solution(mesh):
    placed = (P("seq", "kvh", None), P(), P(), P(None, ("kvh", "rep")), P(("kvh", "rep"), None))
    return jax.shard_map(
        local, mesh=mesh, in_specs=placed, out_specs=P(None, "seq", ("kvh", "rep")), check_vma=False
    )
```

```python
import functools

import jax
import jax.numpy as jnp
from jax import lax
from jax.experimental import pallas as pl
from jax.experimental.pallas import tpu as pltpu
from jax.sharding import PartitionSpec as P

KV_HEADS = 4
HEAD_DIM = 128
GROUP_HEADS = 4


norm_eps = 1e-06
masked_score = -1e30
UNROLL = 16


def layer_norm(states, norm_gain):
    values = states.astype(jnp.float32)
    center = values - jnp.mean(values, axis=-1, keepdims=True)
    spread = jnp.mean(center * center, axis=-1, keepdims=True)
    return (center * lax.rsqrt(spread + norm_eps) * norm_gain).astype(jnp.bfloat16)


def attention_kernel(seq_ref, q_ref, kv_ref, o_ref, *, shards, tok_rows, block):
    seq_index = seq_ref[0]
    scale = HEAD_DIM ** (-0.5)
    blocks = tok_rows // block
    rows = q_ref.shape[0] // blocks
    setups = []
    for qb in range(blocks):
        width = (((qb + 1) * block - 1) // 128 + 1) * 128
        row_j = qb * block + lax.broadcasted_iota(jnp.int32, (rows, 1), 0) % block
        lane_pos = lax.broadcasted_iota(jnp.int32, (1, width), 1) * shards
        setups.append((width, row_j * shards + seq_index, lane_pos))

    def body(src, carry):
        first = pl.multiple_of(src * tok_rows, tok_rows)
        out = []
        for qb in range(blocks):
            width, query_pos, lane_pos = setups[qb]
            top, total, context = carry[qb]
            q = q_ref[qb * rows : (qb + 1) * rows, :]
            key = kv_ref[pl.ds(first, width), :HEAD_DIM]
            value = kv_ref[pl.ds(first, width), HEAD_DIM:]
            scores = lax.dot_general(
                q, key, (((1,), (1,)), ((), ())), preferred_element_type=jnp.float32
            ) * scale
            allowed = lane_pos <= query_pos - src
            scores = jnp.where(allowed, scores, masked_score)
            new_top = jnp.maximum(top, jnp.max(scores, axis=1, keepdims=True))
            shrink = jnp.exp(top - new_top)
            weights = jnp.exp(scores - new_top)
            total = shrink * total + jnp.sum(weights, axis=1, keepdims=True)
            update = jnp.dot(
                weights.astype(jnp.bfloat16), value, preferred_element_type=jnp.float32
            )
            out.append((new_top, total, shrink * context + update))
        return tuple(out)

    start = tuple(
        (
            jnp.full((rows, 1), masked_score, jnp.float32),
            jnp.zeros((rows, 1), jnp.float32),
            jnp.zeros((rows, HEAD_DIM), jnp.float32),
        )
        for _ in range(blocks)
    )
    final = lax.fori_loop(0, shards, body, start, unroll=UNROLL)
    for qb in range(blocks):
        _, total, context = final[qb]
        o_ref[qb * rows : (qb + 1) * rows, :] = (context / total).astype(o_ref.dtype)


def causal_attention(seq_index, queries, pair_all, block=128):
    tok_rows, heads_local, _ = queries.shape
    shards = pair_all.shape[0]
    blocks = tok_rows // block
    q_rows = (
        queries.reshape(blocks, block, heads_local, HEAD_DIM)
        .transpose(0, 2, 1, 3)
        .reshape(tok_rows * heads_local, HEAD_DIM)
    )
    kv_rows = pair_all.reshape(shards * tok_rows, 2 * HEAD_DIM)
    out = pl.pallas_call(
        functools.partial(attention_kernel, shards=shards, tok_rows=tok_rows, block=block),
        out_shape=jax.ShapeDtypeStruct((tok_rows * heads_local, HEAD_DIM), jnp.bfloat16),
        in_specs=[
            pl.BlockSpec(memory_space=pltpu.SMEM),
            pl.BlockSpec(memory_space=pltpu.VMEM),
            pl.BlockSpec(memory_space=pltpu.VMEM),
        ],
        out_specs=pl.BlockSpec(memory_space=pltpu.VMEM),
        compiler_params=pltpu.CompilerParams(vmem_limit_bytes=48 * 1024 * 1024),
        cost_estimate=pl.CostEstimate(
            flops=4 * tok_rows * heads_local * shards * tok_rows * HEAD_DIM * 3 // 4,
            transcendentals=tok_rows * heads_local * shards * tok_rows * 3 // 4,
            bytes_accessed=kv_rows.size * 2 + 2 * q_rows.size * 2,
        ),
    )(jnp.reshape(seq_index, (1,)).astype(jnp.int32), q_rows, kv_rows)
    return (
        out.reshape(blocks, heads_local, block, HEAD_DIM)
        .transpose(0, 2, 1, 3)
        .reshape(tok_rows, 1, heads_local * HEAD_DIM)
    )


def ring_reduce_scatter(parts):
    count = parts.shape[0]
    axes = ("kvh", "rep")
    index = lax.axis_index("kvh") * lax.axis_size("rep") + lax.axis_index("rep")
    half = parts.shape[-1] // 2
    sums = []
    for step_dir, piece in ((1, parts[..., :half]), (-1, parts[..., half:])):
        perm = [(i, (i + step_dir) % count) for i in range(count)]
        buf = lax.dynamic_index_in_dim(piece, (index - step_dir) % count, 0, keepdims=False)
        for t in range(1, count):
            buf = lax.ppermute(buf, axes, perm)
            own = lax.dynamic_index_in_dim(piece, (index - step_dir * (t + 1)) % count, 0, keepdims=False)
            buf = buf + own
        sums.append(buf)
    return jnp.concatenate(sums, axis=-1)


def local(vision_states, frame_tokens, norm_gain, projector, head_weights):
    seq_count = lax.axis_size("seq")
    seq_index = lax.axis_index("seq")
    rep_count = lax.axis_size("rep")
    frames_dev = vision_states.shape[0]
    frame_max = vision_states.shape[1] * lax.axis_size("kvh")
    d_cols = projector.shape[1]
    cap_frame = frame_max // seq_count
    tok_rows = 2 * frames_dev * frame_max // 3
    heads_local = GROUP_HEADS // rep_count
    normed = layer_norm(vision_states, norm_gain)
    frame_rows = lax.all_gather(normed[0], "kvh", axis=0, tiled=False).reshape(1, frame_max, -1)
    hidden = jnp.einsum(
        "frv,vc->frc",
        frame_rows,
        projector,
        preferred_element_type=jnp.float32,
    )
    visual_frames = jax.nn.gelu(hidden, approximate=False).astype(jnp.bfloat16)
    ends = jnp.cumsum(frame_tokens)
    starts_all = ends - frame_tokens
    my_starts = lax.dynamic_slice_in_dim(starts_all, seq_index * frames_dev, frames_dev, 0)
    dest = jnp.arange(seq_count, dtype=jnp.int32)[:, None, None]
    slots = jnp.arange(cap_frame, dtype=jnp.int32)[None, None, :]
    frame_local = jnp.arange(frames_dev, dtype=jnp.int32)[None, :, None]
    row_of = jnp.mod(dest - my_starts[None, :, None], seq_count) + slots * seq_count
    send_index = (frame_local * frame_max + row_of).reshape(-1)
    outgoing = visual_frames.reshape(frames_dev * frame_max, d_cols)[send_index]
    received = lax.all_to_all(outgoing, "seq", split_axis=0, concat_axis=0, tiled=True)
    query_pos = jnp.arange(tok_rows, dtype=jnp.int32) * seq_count + seq_index
    before = ends[None, :] <= query_pos[:, None]
    frame = jnp.sum(before.astype(jnp.int32), axis=1)
    offset = jnp.sum(jnp.where(before, frame_tokens[None, :], 0), axis=1)
    slot_index = frame * cap_frame + (query_pos - offset) // seq_count
    visual = received[slot_index]
    wide = head_weights.reshape(d_cols, KV_HEADS, GROUP_HEADS + 2, HEAD_DIM)
    query_w = wide[:, :, :GROUP_HEADS].reshape(d_cols, KV_HEADS * rep_count, heads_local * HEAD_DIM)
    pair_w = wide[:, :, GROUP_HEADS:].reshape(d_cols, KV_HEADS, 1, 2 * HEAD_DIM)
    pair_w = jnp.broadcast_to(pair_w, (d_cols, KV_HEADS, rep_count, 2 * HEAD_DIM)).reshape(
        d_cols, KV_HEADS * rep_count, 2 * HEAD_DIM
    )
    pair_part = jnp.einsum("tc,cpw->ptw", visual, pair_w, preferred_element_type=jnp.float32)
    pair_own = lax.psum_scatter(
        pair_part, ("kvh", "rep"), scatter_dimension=0, tiled=True
    )[0].astype(jnp.bfloat16)
    query_part = jnp.einsum("tc,cpw->ptw", visual, query_w, preferred_element_type=jnp.float32)
    queries = ring_reduce_scatter(query_part).astype(jnp.bfloat16)
    queries = queries.reshape(tok_rows, heads_local, HEAD_DIM)
    pair_all = lax.all_gather(pair_own, "seq", axis=0, tiled=False)
    return causal_attention(seq_index, queries, pair_all)


def solution(mesh):
    placed = (P("seq", "kvh", None), P(), P(), P(None, ("kvh", "rep")), P(("kvh", "rep"), None))
    return jax.shard_map(
        local, mesh=mesh, in_specs=placed, out_specs=P(None, "seq", ("kvh", "rep")), check_vma=False
    )
```

```python
import functools

import jax
import jax.numpy as jnp
from jax import lax
from jax.experimental import pallas as pl
from jax.experimental.pallas import tpu as pltpu
from jax.sharding import PartitionSpec as P

KV_HEADS = 4
HEAD_DIM = 128
GROUP_HEADS = 4


norm_eps = 1e-06
masked_score = -1e30
UNROLL = 16


def layer_norm(states, norm_gain):
    values = states.astype(jnp.float32)
    center = values - jnp.mean(values, axis=-1, keepdims=True)
    spread = jnp.mean(center * center, axis=-1, keepdims=True)
    return (center * lax.rsqrt(spread + norm_eps) * norm_gain).astype(jnp.bfloat16)


def attention_kernel(seq_ref, q_ref, kv_ref, o_ref, *, shards, tok_rows, block):
    seq_index = seq_ref[0]
    scale = HEAD_DIM ** (-0.5)
    blocks = tok_rows // block
    rows = q_ref.shape[0] // blocks
    setups = []
    for qb in range(blocks):
        width = (((qb + 1) * block - 1) // 128 + 1) * 128
        row_j = qb * block + lax.broadcasted_iota(jnp.int32, (rows, 1), 0) % block
        lane_pos = lax.broadcasted_iota(jnp.int32, (1, width), 1) * shards
        setups.append((width, row_j * shards + seq_index, lane_pos))

    def body(src, carry):
        first = pl.multiple_of(src * tok_rows, tok_rows)
        out = []
        for qb in range(blocks):
            width, query_pos, lane_pos = setups[qb]
            top, total, context = carry[qb]
            q = q_ref[qb * rows : (qb + 1) * rows, :]
            key = kv_ref[pl.ds(first, width), :HEAD_DIM]
            value = kv_ref[pl.ds(first, width), HEAD_DIM:]
            scores = lax.dot_general(
                q, key, (((1,), (1,)), ((), ())), preferred_element_type=jnp.float32
            ) * scale
            free = (qb * block // 128) * 128
            allowed = lane_pos[:, free:] <= query_pos - src
            edge = jnp.where(allowed, scores[:, free:], masked_score)
            scores = jnp.concatenate([scores[:, :free], edge], axis=1) if free else edge
            new_top = jnp.maximum(top, jnp.max(scores, axis=1, keepdims=True))
            shrink = jnp.exp(top - new_top)
            weights = jnp.exp(scores - new_top)
            total = shrink * total + jnp.sum(weights, axis=1, keepdims=True)
            update = jnp.dot(
                weights.astype(jnp.bfloat16), value, preferred_element_type=jnp.float32
            )
            out.append((new_top, total, shrink * context + update))
        return tuple(out)

    start = tuple(
        (
            jnp.full((rows, 1), masked_score, jnp.float32),
            jnp.zeros((rows, 1), jnp.float32),
            jnp.zeros((rows, HEAD_DIM), jnp.float32),
        )
        for _ in range(blocks)
    )
    final = lax.fori_loop(0, shards, body, start, unroll=UNROLL)
    for qb in range(blocks):
        _, total, context = final[qb]
        o_ref[qb * rows : (qb + 1) * rows, :] = (context / total).astype(o_ref.dtype)


def causal_attention(seq_index, queries, pair_all, block=128):
    tok_rows, heads_local, _ = queries.shape
    shards = pair_all.shape[0]
    blocks = tok_rows // block
    q_rows = (
        queries.reshape(blocks, block, heads_local, HEAD_DIM)
        .transpose(0, 2, 1, 3)
        .reshape(tok_rows * heads_local, HEAD_DIM)
    )
    kv_rows = pair_all.reshape(shards * tok_rows, 2 * HEAD_DIM)
    out = pl.pallas_call(
        functools.partial(attention_kernel, shards=shards, tok_rows=tok_rows, block=block),
        out_shape=jax.ShapeDtypeStruct((tok_rows * heads_local, HEAD_DIM), jnp.bfloat16),
        in_specs=[
            pl.BlockSpec(memory_space=pltpu.SMEM),
            pl.BlockSpec(memory_space=pltpu.VMEM),
            pl.BlockSpec(memory_space=pltpu.VMEM),
        ],
        out_specs=pl.BlockSpec(memory_space=pltpu.VMEM),
        compiler_params=pltpu.CompilerParams(vmem_limit_bytes=48 * 1024 * 1024),
        cost_estimate=pl.CostEstimate(
            flops=4 * tok_rows * heads_local * shards * tok_rows * HEAD_DIM * 3 // 4,
            transcendentals=tok_rows * heads_local * shards * tok_rows * 3 // 4,
            bytes_accessed=kv_rows.size * 2 + 2 * q_rows.size * 2,
        ),
    )(jnp.reshape(seq_index, (1,)).astype(jnp.int32), q_rows, kv_rows)
    return (
        out.reshape(blocks, heads_local, block, HEAD_DIM)
        .transpose(0, 2, 1, 3)
        .reshape(tok_rows, 1, heads_local * HEAD_DIM)
    )


def ring_reduce_scatter(parts):
    count = parts.shape[0]
    axes = ("kvh", "rep")
    index = lax.axis_index("kvh") * lax.axis_size("rep") + lax.axis_index("rep")
    half = parts.shape[-1] // 2
    sums = []
    for step_dir, piece in ((1, parts[..., :half]), (-1, parts[..., half:])):
        perm = [(i, (i + step_dir) % count) for i in range(count)]
        buf = lax.dynamic_index_in_dim(piece, (index - step_dir) % count, 0, keepdims=False)
        for t in range(1, count):
            buf = lax.ppermute(buf, axes, perm)
            own = lax.dynamic_index_in_dim(piece, (index - step_dir * (t + 1)) % count, 0, keepdims=False)
            buf = buf + own
        sums.append(buf)
    return jnp.concatenate(sums, axis=-1)


def local(vision_states, frame_tokens, norm_gain, projector, head_weights):
    seq_count = lax.axis_size("seq")
    seq_index = lax.axis_index("seq")
    rep_count = lax.axis_size("rep")
    frames_dev = vision_states.shape[0]
    frame_max = vision_states.shape[1] * lax.axis_size("kvh")
    d_cols = projector.shape[1]
    cap_frame = frame_max // seq_count
    tok_rows = 2 * frames_dev * frame_max // 3
    heads_local = GROUP_HEADS // rep_count
    normed = layer_norm(vision_states, norm_gain)
    frame_rows = lax.all_gather(normed[0], "kvh", axis=0, tiled=False).reshape(1, frame_max, -1)
    hidden = jnp.einsum(
        "frv,vc->frc",
        frame_rows,
        projector,
        preferred_element_type=jnp.float32,
    )
    visual_frames = jax.nn.gelu(hidden, approximate=False).astype(jnp.bfloat16)
    ends = jnp.cumsum(frame_tokens)
    starts_all = ends - frame_tokens
    my_starts = lax.dynamic_slice_in_dim(starts_all, seq_index * frames_dev, frames_dev, 0)
    dest = jnp.arange(seq_count, dtype=jnp.int32)[:, None, None]
    slots = jnp.arange(cap_frame, dtype=jnp.int32)[None, None, :]
    frame_local = jnp.arange(frames_dev, dtype=jnp.int32)[None, :, None]
    row_of = jnp.mod(dest - my_starts[None, :, None], seq_count) + slots * seq_count
    send_index = (frame_local * frame_max + row_of).reshape(-1)
    outgoing = visual_frames.reshape(frames_dev * frame_max, d_cols)[send_index]
    received = lax.all_to_all(outgoing, "seq", split_axis=0, concat_axis=0, tiled=True)
    query_pos = jnp.arange(tok_rows, dtype=jnp.int32) * seq_count + seq_index
    before = ends[None, :] <= query_pos[:, None]
    frame = jnp.sum(before.astype(jnp.int32), axis=1)
    offset = jnp.sum(jnp.where(before, frame_tokens[None, :], 0), axis=1)
    slot_index = frame * cap_frame + (query_pos - offset) // seq_count
    visual = received[slot_index]
    wide = head_weights.reshape(d_cols, KV_HEADS, GROUP_HEADS + 2, HEAD_DIM)
    query_w = wide[:, :, :GROUP_HEADS].reshape(d_cols, KV_HEADS * rep_count, heads_local * HEAD_DIM)
    pair_w = wide[:, :, GROUP_HEADS:].reshape(d_cols, KV_HEADS, 1, 2 * HEAD_DIM)
    pair_w = jnp.broadcast_to(pair_w, (d_cols, KV_HEADS, rep_count, 2 * HEAD_DIM)).reshape(
        d_cols, KV_HEADS * rep_count, 2 * HEAD_DIM
    )
    pair_part = jnp.einsum("tc,cpw->ptw", visual, pair_w, preferred_element_type=jnp.float32)
    pair_own = lax.psum_scatter(
        pair_part, ("kvh", "rep"), scatter_dimension=0, tiled=True
    )[0].astype(jnp.bfloat16)
    query_part = jnp.einsum("tc,cpw->ptw", visual, query_w, preferred_element_type=jnp.float32)
    queries = ring_reduce_scatter(query_part).astype(jnp.bfloat16)
    queries = queries.reshape(tok_rows, heads_local, HEAD_DIM)
    pair_all = lax.all_gather(pair_own, "seq", axis=0, tiled=False)
    return causal_attention(seq_index, queries, pair_all)


def solution(mesh):
    placed = (P("seq", "kvh", None), P(), P(), P(None, ("kvh", "rep")), P(("kvh", "rep"), None))
    return jax.shard_map(
        local, mesh=mesh, in_specs=placed, out_specs=P(None, "seq", ("kvh", "rep")), check_vma=False
    )
```

```python
import functools

import jax
import jax.numpy as jnp
from jax import lax
from jax.experimental import pallas as pl
from jax.experimental.pallas import tpu as pltpu
from jax.sharding import PartitionSpec as P

KV_HEADS = 4
HEAD_DIM = 128
GROUP_HEADS = 4


norm_eps = 1e-06
masked_score = -1e30
UNROLL = 16


def layer_norm(states, norm_gain):
    values = states.astype(jnp.float32)
    center = values - jnp.mean(values, axis=-1, keepdims=True)
    spread = jnp.mean(center * center, axis=-1, keepdims=True)
    return (center * lax.rsqrt(spread + norm_eps) * norm_gain).astype(jnp.bfloat16)


def attention_kernel(seq_ref, q_ref, kv_ref, o_ref, *, shards, tok_rows, block):
    seq_index = seq_ref[0]
    scale = HEAD_DIM ** (-0.5)
    blocks = tok_rows // block
    rows = q_ref.shape[0] // blocks
    setups = []
    for qb in range(blocks):
        width = (((qb + 1) * block - 1) // 128 + 1) * 128
        row_j = qb * block + lax.broadcasted_iota(jnp.int32, (rows, 1), 0) % block
        lane_pos = lax.broadcasted_iota(jnp.int32, (1, width), 1) * shards
        setups.append((width, row_j * shards + seq_index, lane_pos))

    def body(src, carry):
        first = pl.multiple_of(src * tok_rows, tok_rows)
        out = []
        for qb in range(blocks):
            width, query_pos, lane_pos = setups[qb]
            top, total, context = carry[qb]
            q = q_ref[qb * rows : (qb + 1) * rows, :]
            key = kv_ref[pl.ds(first, width), :HEAD_DIM]
            value = kv_ref[pl.ds(first, width), HEAD_DIM:]
            scores = lax.dot_general(
                q, key, (((1,), (1,)), ((), ())), preferred_element_type=jnp.float32
            ) * scale
            free = (qb * block // 128) * 128
            allowed = lane_pos[:, free:] <= query_pos - src
            edge = jnp.where(allowed, scores[:, free:], masked_score)
            scores = jnp.concatenate([scores[:, :free], edge], axis=1) if free else edge
            new_top = jnp.maximum(top, jnp.max(scores, axis=1, keepdims=True))
            shrink = jnp.exp(top - new_top)
            weights = jnp.exp(scores - new_top)
            total = shrink * total + jnp.sum(weights, axis=1, keepdims=True)
            update = jnp.dot(
                weights.astype(jnp.bfloat16), value, preferred_element_type=jnp.float32
            )
            out.append((new_top, total, shrink * context + update))
        return tuple(out)

    start = tuple(
        (
            jnp.full((rows, 1), masked_score, jnp.float32),
            jnp.zeros((rows, 1), jnp.float32),
            jnp.zeros((rows, HEAD_DIM), jnp.float32),
        )
        for _ in range(blocks)
    )
    final = lax.fori_loop(0, shards, body, start, unroll=UNROLL)
    heads = rows // block
    for qb in range(blocks):
        _, total, context = final[qb]
        result = (context / total).astype(o_ref.dtype)
        for h in range(heads):
            o_ref[qb * block : (qb + 1) * block, h * HEAD_DIM : (h + 1) * HEAD_DIM] = result[
                h * block : (h + 1) * block
            ]


def causal_attention(seq_index, queries, pair_all, block=128):
    tok_rows, heads_local, _ = queries.shape
    shards = pair_all.shape[0]
    blocks = tok_rows // block
    q_rows = (
        queries.reshape(blocks, block, heads_local, HEAD_DIM)
        .transpose(0, 2, 1, 3)
        .reshape(tok_rows * heads_local, HEAD_DIM)
    )
    kv_rows = pair_all.reshape(shards * tok_rows, 2 * HEAD_DIM)
    out = pl.pallas_call(
        functools.partial(attention_kernel, shards=shards, tok_rows=tok_rows, block=block),
        out_shape=jax.ShapeDtypeStruct((tok_rows, heads_local * HEAD_DIM), jnp.bfloat16),
        in_specs=[
            pl.BlockSpec(memory_space=pltpu.SMEM),
            pl.BlockSpec(memory_space=pltpu.VMEM),
            pl.BlockSpec(memory_space=pltpu.VMEM),
        ],
        out_specs=pl.BlockSpec(memory_space=pltpu.VMEM),
        compiler_params=pltpu.CompilerParams(vmem_limit_bytes=48 * 1024 * 1024),
        cost_estimate=pl.CostEstimate(
            flops=4 * tok_rows * heads_local * shards * tok_rows * HEAD_DIM * 3 // 4,
            transcendentals=tok_rows * heads_local * shards * tok_rows * 3 // 4,
            bytes_accessed=kv_rows.size * 2 + 2 * q_rows.size * 2,
        ),
    )(jnp.reshape(seq_index, (1,)).astype(jnp.int32), q_rows, kv_rows)
    return out.reshape(tok_rows, 1, heads_local * HEAD_DIM)


def ring_reduce_scatter(parts):
    count = parts.shape[0]
    axes = ("kvh", "rep")
    index = lax.axis_index("kvh") * lax.axis_size("rep") + lax.axis_index("rep")
    half = parts.shape[-1] // 2
    sums = []
    for step_dir, piece in ((1, parts[..., :half]), (-1, parts[..., half:])):
        perm = [(i, (i + step_dir) % count) for i in range(count)]
        buf = lax.dynamic_index_in_dim(piece, (index - step_dir) % count, 0, keepdims=False)
        for t in range(1, count):
            buf = lax.ppermute(buf, axes, perm)
            own = lax.dynamic_index_in_dim(piece, (index - step_dir * (t + 1)) % count, 0, keepdims=False)
            buf = buf + own
        sums.append(buf)
    return jnp.concatenate(sums, axis=-1)


def local(vision_states, frame_tokens, norm_gain, projector, head_weights):
    seq_count = lax.axis_size("seq")
    seq_index = lax.axis_index("seq")
    rep_count = lax.axis_size("rep")
    frames_dev = vision_states.shape[0]
    frame_max = vision_states.shape[1] * lax.axis_size("kvh")
    d_cols = projector.shape[1]
    cap_frame = frame_max // seq_count
    tok_rows = 2 * frames_dev * frame_max // 3
    heads_local = GROUP_HEADS // rep_count
    normed = layer_norm(vision_states, norm_gain)
    frame_rows = lax.all_gather(normed[0], "kvh", axis=0, tiled=False).reshape(1, frame_max, -1)
    hidden = jnp.einsum(
        "frv,vc->frc",
        frame_rows,
        projector,
        preferred_element_type=jnp.float32,
    )
    visual_frames = jax.nn.gelu(hidden, approximate=False).astype(jnp.bfloat16)
    ends = jnp.cumsum(frame_tokens)
    starts_all = ends - frame_tokens
    my_starts = lax.dynamic_slice_in_dim(starts_all, seq_index * frames_dev, frames_dev, 0)
    dest = jnp.arange(seq_count, dtype=jnp.int32)[:, None, None]
    slots = jnp.arange(cap_frame, dtype=jnp.int32)[None, None, :]
    frame_local = jnp.arange(frames_dev, dtype=jnp.int32)[None, :, None]
    row_of = jnp.mod(dest - my_starts[None, :, None], seq_count) + slots * seq_count
    send_index = (frame_local * frame_max + row_of).reshape(-1)
    outgoing = visual_frames.reshape(frames_dev * frame_max, d_cols)[send_index]
    received = lax.all_to_all(outgoing, "seq", split_axis=0, concat_axis=0, tiled=True)
    query_pos = jnp.arange(tok_rows, dtype=jnp.int32) * seq_count + seq_index
    before = ends[None, :] <= query_pos[:, None]
    frame = jnp.sum(before.astype(jnp.int32), axis=1)
    offset = jnp.sum(jnp.where(before, frame_tokens[None, :], 0), axis=1)
    slot_index = frame * cap_frame + (query_pos - offset) // seq_count
    visual = received[slot_index]
    wide = head_weights.reshape(d_cols, KV_HEADS, GROUP_HEADS + 2, HEAD_DIM)
    query_w = wide[:, :, :GROUP_HEADS].reshape(d_cols, KV_HEADS * rep_count, heads_local * HEAD_DIM)
    pair_w = wide[:, :, GROUP_HEADS:].reshape(d_cols, KV_HEADS, 1, 2 * HEAD_DIM)
    pair_w = jnp.broadcast_to(pair_w, (d_cols, KV_HEADS, rep_count, 2 * HEAD_DIM)).reshape(
        d_cols, KV_HEADS * rep_count, 2 * HEAD_DIM
    )
    pair_part = jnp.einsum("tc,cpw->ptw", visual, pair_w, preferred_element_type=jnp.float32)
    pair_own = lax.psum_scatter(
        pair_part, ("kvh", "rep"), scatter_dimension=0, tiled=True
    )[0].astype(jnp.bfloat16)
    query_part = jnp.einsum("tc,cpw->ptw", visual, query_w, preferred_element_type=jnp.float32)
    queries = ring_reduce_scatter(query_part).astype(jnp.bfloat16)
    queries = queries.reshape(tok_rows, heads_local, HEAD_DIM)
    pair_all = lax.all_gather(pair_own, "seq", axis=0, tiled=False)
    return causal_attention(seq_index, queries, pair_all)


def solution(mesh):
    placed = (P("seq", "kvh", None), P(), P(), P(None, ("kvh", "rep")), P(("kvh", "rep"), None))
    return jax.shard_map(
        local, mesh=mesh, in_specs=placed, out_specs=P(None, "seq", ("kvh", "rep")), check_vma=False
    )
```
